32 devices in a mesh: seq: 8 (over z, y), head: 4 (over x, core).
Axes of the slice: x: 2, y: 2, z: 4, core: 2. Of those that a mesh axis runs over, the one named last changes fastest.
Arguments:
- queries: bfloat16 [2048, 4096], P(('seq', 'head')), may hold values from -120 to 120
- key_rows: bfloat16 [2048, 4096], P(('seq', 'head')), may hold values from -24 to 24
- value_rows: bfloat16 [2048, 4096], P(('seq', 'head')), may hold values from -6 to 6
- out_grad: bfloat16 [2048, 4096], P(('seq', 'head')), may hold values from -6 to 6
- summary_columns: int32 [16, 8], P('seq'), may hold values from 0 to 127, as said below
Outputs:
- attended: bfloat16 [2048, 4096], P(('seq', 'head'))
- query_grad: bfloat16 [2048, 4096], P(('seq', 'head'))
- key_grad: bfloat16 [2048, 4096], P(('seq', 'head'))
- value_grad: bfloat16 [2048, 4096], P(('seq', 'head'))
The draws below stay inside these ranges and needn't reach their ends.
Inputs may be any that keep to these rules, and one draw needn't show every extreme that they name: `summary_columns`: in each block the 8 columns are distinct and increasing, and the last one is always 128 - 1.
All inputs are finite; a program needn't handle non-finite values.
Results may differ from the reference program's by a relative error of at most 0.025.
Values may be sent and summed in bfloat16 or wider, within the bound.
No kernel may reach another device: no remote copies, remote signals or barrier semaphores. Data moves between devices by JAX's collectives and lax.ppermute only.
A program may use at most 128 MiB of HBM per device.

```python
import math
import jax
import jax.numpy as jnp
from jax import lax

HEADS = 32
HEAD_DIM = 128
BLOCK = 128
SUMMARY = 8
TOK_DEV = 256
TOKENS = 2048
BLOCKS = 16
SUMS = 128
FEATS = 4096
N_SEQ = 8


def shared_fields(key):
    dims_all = (TOKENS, HEADS * HEAD_DIM)
    base_key = jax.random.fold_in(key, 101)
    query_key = jax.random.fold_in(key, 102)
    raw_keys = jax.random.normal(base_key, dims_all, jnp.float32)
    key_field = 1.25 * raw_keys
    query_field = 1.25 * jax.random.normal(query_key, dims_all, jnp.float32)
    return (jnp.clip(query_field, -120.0, 120.0), jnp.clip(key_field, -24.0, 24.0))


def draw_queries(key, part):
    return shared_fields(key)[0].astype(jnp.bfloat16)


def draw_key_rows(key, part):
    return shared_fields(key)[1].astype(jnp.bfloat16)


def draw_summary_columns(key, part):
    own_key = jax.random.fold_in(key, 201)
    block_keys = jax.random.split(own_key, BLOCKS)
    picked = jax.vmap(lambda one_key: jax.random.permutation(one_key, BLOCK - 1)[:SUMMARY - 1])(block_keys)
    ordered = jnp.sort(picked, axis=1).astype(jnp.int32)
    last_column = jnp.full((BLOCKS, 1), BLOCK - 1, jnp.int32)
    return jnp.concatenate([ordered, last_column], axis=1)


def block_scale(key, shape, shards, least, largest):
    level = 1.0
    for dim, parts in shards:
        heights = jax.random.uniform(jax.random.fold_in(jax.random.fold_in(key, 6), dim), (parts,), jnp.float32, least / len(shards), largest / len(shards))
        level = level * jnp.repeat(jnp.exp(heights), shape[dim] // parts).reshape((-1,) + (1,) * (len(shape) - 1 - dim))
    return level


def gaussian(key, dims, deviation, most, cuts=(), kind=jnp.bfloat16):
    drawn = deviation * jax.random.normal(key, dims, jnp.float32)
    if cuts:
        drawn = drawn * block_scale(key, dims, cuts, -0.22, 0.18)
    return jnp.clip(drawn, -most, most).astype(kind)


def setup_inputs(seed: int = 0) -> dict:
    seeds = jax.random.split(jax.random.key(seed), 6)
    queries = draw_queries(jax.random.fold_in(seeds[5], 71), 0)
    key_rows = draw_key_rows(jax.random.fold_in(seeds[5], 71), 0)
    value_rows = gaussian(seeds[2], (TOKENS, FEATS), 1.0, 6.0, ((0, 32),))
    out_grad = gaussian(seeds[3], (TOKENS, FEATS), 1.0, 6.0, ((0, 32),))
    summary_columns = draw_summary_columns(jax.random.fold_in(seeds[5], 71), 0)
    return dict(queries=queries, key_rows=key_rows, value_rows=value_rows, out_grad=out_grad, summary_columns=summary_columns)


MASKED_SCORE = -1e+30

def as_float(array):
    return array.astype(jnp.float32)

def rounded(array):
    return lax.optimization_barrier(array.astype(jnp.bfloat16)).astype(jnp.float32)

def take_rows(source, row_offset, count):
    return lax.dynamic_slice_in_dim(source, row_offset, count, 0)

def put_rows(target, update, row_offset):
    return lax.dynamic_update_slice_in_dim(target, update, row_offset, 0)

def pair_sweep(row_block, key_block, row_size, key_size, visit_fn, initial):
    row_tiles = row_block.shape[0] // row_size
    key_tiles = key_block.shape[0] // key_size

    def visit_pair(pair_index, current):
        row_start = (pair_index // key_tiles * row_size).astype(jnp.int32)
        key_start = (pair_index % key_tiles * key_size).astype(jnp.int32)
        newest = jnp.max(take_rows(row_block, row_start, row_size))
        oldest = take_rows(key_block, key_start, 1)[0]
        return lax.cond(oldest < newest, lambda held_state: visit_fn(held_state, row_start, key_start), lambda held_state: held_state, current)
    return lax.fori_loop(0, row_tiles * key_tiles, visit_pair, initial)

def tile_mask(row_block, key_block, row_start, key_start, row_size, key_size):
    row_part = take_rows(row_block, row_start, row_size)
    key_part = take_rows(key_block, key_start, key_size)
    return (key_part[None, :] < row_part[:, None])[:, None, :]

def tile_scores(query_heads, sum_keys, row_start, key_start, row_size, key_size, score_scale):
    query_tile = take_rows(query_heads, row_start, row_size)
    key_tile = take_rows(sum_keys, key_start, key_size)
    return jnp.einsum('rhd,khd->rhk', query_tile, key_tile) * score_scale

def joint_norm(first_max, first_total, second_max, second_total):
    highest = jnp.maximum(first_max, second_max)
    return highest + jnp.log(first_total * jnp.exp(first_max - highest) + second_total * jnp.exp(second_max - highest))

def reference(queries, key_rows, value_rows, out_grad, summary_columns):
    feature_count = HEADS * HEAD_DIM
    score_scale = 1.0 / math.sqrt(HEAD_DIM)
    block_count = TOK_DEV // BLOCK
    positions = (jnp.arange(BLOCKS, dtype=jnp.int32)[:, None] * BLOCK + summary_columns).reshape(-1).astype(jnp.int32)
    sum_keys = as_float(jnp.take(key_rows, positions, axis=0)).reshape(SUMS, HEADS, HEAD_DIM)
    sum_values = as_float(jnp.take(value_rows, positions, axis=0)).reshape(SUMS, HEADS, HEAD_DIM)
    key_block = jnp.arange(SUMS, dtype=jnp.int32) // SUMMARY
    row_size = math.gcd(TOK_DEV, 64)
    key_size = math.gcd(SUMS, 256)
    span_index = jnp.arange(BLOCK, dtype=jnp.int32)
    causal = (span_index[:, None] >= span_index[None, :])[None, :, None, :]

    def shard_step(carried, shard_index):
        key_part, value_part = carried
        row_offset = (shard_index * TOK_DEV).astype(jnp.int32)
        query_heads = as_float(take_rows(queries, row_offset, TOK_DEV)).reshape(TOK_DEV, HEADS, HEAD_DIM)
        key_heads = as_float(take_rows(key_rows, row_offset, TOK_DEV)).reshape(TOK_DEV, HEADS, HEAD_DIM)
        value_heads = as_float(take_rows(value_rows, row_offset, TOK_DEV)).reshape(TOK_DEV, HEADS, HEAD_DIM)
        grad_heads = as_float(take_rows(out_grad, row_offset, TOK_DEV)).reshape(TOK_DEV, HEADS, HEAD_DIM)
        row_block = (row_offset + jnp.arange(TOK_DEV, dtype=jnp.int32)) // BLOCK
        query_blocks = query_heads.reshape(block_count, BLOCK, HEADS, HEAD_DIM)
        key_blocks = key_heads.reshape(block_count, BLOCK, HEADS, HEAD_DIM)
        value_blocks = value_heads.reshape(block_count, BLOCK, HEADS, HEAD_DIM)
        grad_blocks = grad_heads.reshape(block_count, BLOCK, HEADS, HEAD_DIM)
        window_raw = jnp.einsum('bihd,bjhd->bihj', query_blocks, key_blocks) * score_scale
        window_scores = jnp.where(causal, window_raw, MASKED_SCORE)
        window_max = lax.optimization_barrier(jnp.max(window_scores, axis=3))
        window_total = lax.optimization_barrier(jnp.sum(jnp.where(causal, jnp.exp(window_scores - window_max[..., None]), 0.0), axis=3))

        def stats_visit(running, row_start, key_start):
            run_max, run_total = running
            allowed = tile_mask(row_block, key_block, row_start, key_start, row_size, key_size)
            scores = jnp.where(allowed, tile_scores(query_heads, sum_keys, row_start, key_start, row_size, key_size, score_scale), MASKED_SCORE)
            old_max = take_rows(run_max, row_start, row_size)
            new_max = jnp.maximum(old_max, lax.optimization_barrier(jnp.max(scores, axis=2)))
            weights = jnp.where(allowed, jnp.exp(scores - new_max[:, :, None]), 0.0)
            new_total = take_rows(run_total, row_start, row_size) * jnp.exp(old_max - new_max) + lax.optimization_barrier(jnp.sum(weights, axis=2))
            return (put_rows(run_max, new_max, row_start), put_rows(run_total, new_total, row_start))
        start_max = jnp.full((TOK_DEV, HEADS), MASKED_SCORE, jnp.float32)
        start_total = jnp.zeros((TOK_DEV, HEADS), jnp.float32)
        sum_max, sum_total = pair_sweep(row_block, key_block, row_size, key_size, stats_visit, (start_max, start_total))
        log_norm = joint_norm(window_max.reshape(TOK_DEV, HEADS), window_total.reshape(TOK_DEV, HEADS), sum_max, sum_total)

        def output_visit(totals, row_start, key_start):
            allowed = tile_mask(row_block, key_block, row_start, key_start, row_size, key_size)
            scores = tile_scores(query_heads, sum_keys, row_start, key_start, row_size, key_size, score_scale)
            norm_part = take_rows(log_norm, row_start, row_size)
            weights_low = rounded(jnp.where(allowed, jnp.exp(scores - norm_part[:, :, None]), 0.0))
            added = jnp.einsum('rhk,khd->rhd', weights_low, take_rows(sum_values, key_start, key_size))
            return put_rows(totals, take_rows(totals, row_start, row_size) + added, row_start)
        summary_part = pair_sweep(row_block, key_block, row_size, key_size, output_visit, jnp.zeros((TOK_DEV, HEADS, HEAD_DIM), jnp.float32))
        norm_blocks = log_norm.reshape(block_count, BLOCK, HEADS)
        window_full = jnp.where(causal, jnp.exp(window_scores - norm_blocks[..., None]), 0.0)
        window_low = rounded(window_full)
        window_out = jnp.einsum('bihj,bjhd->bihd', window_low, value_blocks).reshape(TOK_DEV, HEADS, HEAD_DIM)
        attended_rows = (window_out + summary_part).astype(jnp.bfloat16)
        grad_dot = lax.optimization_barrier(jnp.sum(grad_heads * as_float(attended_rows), axis=2))

        def backward_visit(running, row_start, key_start):
            query_acc, key_acc, value_acc = running
            allowed = tile_mask(row_block, key_block, row_start, key_start, row_size, key_size)
            scores = tile_scores(query_heads, sum_keys, row_start, key_start, row_size, key_size, score_scale)
            weights_full = jnp.where(allowed, jnp.exp(scores - take_rows(log_norm, row_start, row_size)[:, :, None]), 0.0)
            query_tile = take_rows(query_heads, row_start, row_size)
            grad_tile = take_rows(grad_heads, row_start, row_size)
            key_tile = take_rows(sum_keys, key_start, key_size)
            value_tile = take_rows(sum_values, key_start, key_size)
            grad_weights = jnp.einsum('rhd,khd->rhk', grad_tile, value_tile)
            grad_scores = rounded(weights_full * (grad_weights - take_rows(grad_dot, row_start, row_size)[:, :, None]))
            query_add = jnp.einsum('rhk,khd->rhd', grad_scores, key_tile) * score_scale
            key_add = jnp.einsum('rhk,rhd->khd', grad_scores, query_tile) * score_scale
            value_add = jnp.einsum('rhk,rhd->khd', rounded(weights_full), grad_tile)
            query_acc = put_rows(query_acc, take_rows(query_acc, row_start, row_size) + query_add, row_start)
            key_acc = put_rows(key_acc, take_rows(key_acc, key_start, key_size) + key_add, key_start)
            value_acc = put_rows(value_acc, take_rows(value_acc, key_start, key_size) + value_add, key_start)
            return (query_acc, key_acc, value_acc)
        summary_query, key_part, value_part = pair_sweep(row_block, key_block, row_size, key_size, backward_visit, (jnp.zeros((TOK_DEV, HEADS, HEAD_DIM), jnp.float32), key_part, value_part))
        grad_dot_blocks = grad_dot.reshape(block_count, BLOCK, HEADS)
        grad_window = jnp.einsum('bihd,bjhd->bihj', grad_blocks, value_blocks)
        window_dscore = rounded(window_full * (grad_window - grad_dot_blocks[..., None]))
        window_query = jnp.einsum('bihj,bjhd->bihd', window_dscore, key_blocks) * score_scale
        window_key = jnp.einsum('bihj,bihd->bjhd', window_dscore, query_blocks) * score_scale
        window_value = jnp.einsum('bihj,bihd->bjhd', window_low, grad_blocks)
        query_rows = (window_query.reshape(TOK_DEV, feature_count) + summary_query.reshape(TOK_DEV, feature_count)).astype(jnp.bfloat16)
        outputs = (attended_rows.reshape(TOK_DEV, feature_count), query_rows, window_key.reshape(TOK_DEV, feature_count), window_value.reshape(TOK_DEV, feature_count))
        return ((key_part, value_part), outputs)
    initial = (jnp.zeros((SUMS, HEADS, HEAD_DIM), jnp.float32), jnp.zeros((SUMS, HEADS, HEAD_DIM), jnp.float32))
    final_parts, stacked = lax.scan(shard_step, initial, jnp.arange(N_SEQ, dtype=jnp.int32))
    attended = stacked[0].reshape(TOKENS, feature_count)
    query_grad = stacked[1].reshape(TOKENS, feature_count)
    key_grad = stacked[2].reshape(TOKENS, feature_count).at[positions].add(final_parts[0].reshape(SUMS, feature_count)).astype(jnp.bfloat16)
    value_grad = stacked[3].reshape(TOKENS, feature_count).at[positions].add(final_parts[1].reshape(SUMS, feature_count)).astype(jnp.bfloat16)
    return (attended, query_grad, key_grad, value_grad)
```

```python
import math

import jax
import jax.numpy as jnp
from jax import lax
from jax.sharding import Mesh
from jax.sharding import PartitionSpec as P

HEAD_DIM = 128
BLOCK = 128
SUMMARY = 8

MASKED_SCORE = -1e30
GROUP = ("seq", "hx")


def swap_with_partner(x):
    return lax.ppermute(x, "hc", [(0, 1), (1, 0)])


def to_block_layout(arrays, core):
    rows, feats = arrays[0].shape
    half = feats // 2
    mine = [lax.dynamic_slice_in_dim(a, core * half, half, 1) for a in arrays]
    theirs = [lax.dynamic_slice_in_dim(a, (1 - core) * half, half, 1) for a in arrays]
    got = swap_with_partner(jnp.concatenate(theirs, axis=1))
    out = []
    for i, m in enumerate(mine):
        r = got[:, i * half:(i + 1) * half]
        out.append(jnp.where(core == 0, jnp.concatenate([m, r], 0), jnp.concatenate([r, m], 0)))
    return out


def to_token_layout(arrays, core):
    rows2, half = arrays[0].shape
    rows = rows2 // 2
    mine = [lax.dynamic_slice_in_dim(a, core * rows, rows, 0) for a in arrays]
    theirs = [lax.dynamic_slice_in_dim(a, (1 - core) * rows, rows, 0) for a in arrays]
    got = swap_with_partner(jnp.concatenate(theirs, axis=1))
    out = []
    for i, m in enumerate(mine):
        r = got[:, i * half:(i + 1) * half]
        out.append(jnp.where(core == 0, jnp.concatenate([m, r], 1), jnp.concatenate([r, m], 1)))
    return out


def body(queries, key_rows, value_rows, out_grad, summary_columns):
    core = lax.axis_index("hc")
    hx = lax.axis_index("hx")
    shard = lax.axis_index("seq")
    score_scale = 1.0 / math.sqrt(HEAD_DIM)
    f32 = jnp.float32

    qb, kb, vb, gb = to_block_layout([queries, key_rows, value_rows, out_grad], core)
    rows, half = qb.shape
    heads = half // HEAD_DIM
    nb = rows // BLOCK
    pair_count = summary_columns.shape[0] // nb
    first_block = (shard * pair_count + hx) * nb
    cols = lax.dynamic_slice_in_dim(summary_columns, hx * nb, nb, 0)
    positions = (jnp.arange(nb, dtype=jnp.int32)[:, None] * BLOCK + cols).reshape(-1)

    own_sum = jnp.concatenate([jnp.take(kb, positions, axis=0), jnp.take(vb, positions, axis=0)], axis=1)
    all_sum = lax.all_gather(own_sum, GROUP, axis=0, tiled=True)
    sum_count = all_sum.shape[0]
    sk = all_sum[:, :half].reshape(sum_count, heads, HEAD_DIM)
    sv = all_sum[:, half:].reshape(sum_count, heads, HEAD_DIM)

    q = qb.reshape(nb, BLOCK, heads, HEAD_DIM)
    k = kb.reshape(nb, BLOCK, heads, HEAD_DIM)
    v = vb.reshape(nb, BLOCK, heads, HEAD_DIM)
    g = gb.reshape(nb, BLOCK, heads, HEAD_DIM)

    span = jnp.arange(BLOCK, dtype=jnp.int32)
    causal = (span[:, None] >= span[None, :])[None, None]
    key_block = jnp.arange(sum_count, dtype=jnp.int32) // SUMMARY
    query_block = first_block + jnp.arange(nb, dtype=jnp.int32)
    allowed = (key_block[None, :] < query_block[:, None])[:, None, None, :]

    sw = jnp.einsum("bqhd,bkhd->bhqk", q, k, preferred_element_type=f32) * score_scale
    ss = jnp.einsum("bqhd,khd->bhqk", q, sk, preferred_element_type=f32) * score_scale
    sw = jnp.where(causal, sw, MASKED_SCORE)
    ss = jnp.where(allowed, ss, MASKED_SCORE)
    top = jnp.maximum(jnp.max(sw, axis=3), jnp.max(ss, axis=3))
    ew = jnp.where(causal, jnp.exp(sw - top[..., None]), 0.0)
    es = jnp.where(allowed, jnp.exp(ss - top[..., None]), 0.0)
    log_norm = top + jnp.log(jnp.sum(ew, axis=3) + jnp.sum(es, axis=3))
    pw = jnp.where(causal, jnp.exp(sw - log_norm[..., None]), 0.0)
    ps = jnp.where(allowed, jnp.exp(ss - log_norm[..., None]), 0.0)
    pw_low = pw.astype(jnp.bfloat16)
    ps_low = ps.astype(jnp.bfloat16)
    att = jnp.einsum("bhqk,bkhd->bqhd", pw_low, v, preferred_element_type=f32) + jnp.einsum(
        "bhqk,khd->bqhd", ps_low, sv, preferred_element_type=f32
    )
    attended = att.astype(jnp.bfloat16)
    delta = jnp.einsum("bqhd,bqhd->bhq", g.astype(f32), attended.astype(f32), precision=lax.Precision.HIGHEST)

    dpw = jnp.einsum("bqhd,bkhd->bhqk", g, v, preferred_element_type=f32)
    dps = jnp.einsum("bqhd,khd->bhqk", g, sv, preferred_element_type=f32)
    dsw = (pw * (dpw - delta[..., None])).astype(jnp.bfloat16)
    dss = (ps * (dps - delta[..., None])).astype(jnp.bfloat16)
    dq = (
        jnp.einsum("bhqk,bkhd->bqhd", dsw, k, preferred_element_type=f32)
        + jnp.einsum("bhqk,khd->bqhd", dss, sk, preferred_element_type=f32)
    ) * score_scale
    dkw = jnp.einsum("bhqk,bqhd->bkhd", dsw, q, preferred_element_type=f32) * score_scale
    dvw = jnp.einsum("bhqk,bqhd->bkhd", pw_low, g, preferred_element_type=f32)
    dks = jnp.einsum("bhqk,bqhd->khd", dss, q, preferred_element_type=f32) * score_scale
    dvs = jnp.einsum("bhqk,bqhd->khd", ps_low, g, preferred_element_type=f32)

    att_tok, dq_tok = to_token_layout(
        [attended.reshape(rows, half), dq.astype(jnp.bfloat16).reshape(rows, half)], core
    )

    parts = jnp.concatenate([dks.reshape(sum_count, half), dvs.reshape(sum_count, half)], axis=1)
    own_grad = lax.psum_scatter(parts, GROUP, scatter_dimension=0, tiled=True)
    dk = dkw.reshape(rows, half).at[positions].add(own_grad[:, :half])
    dv = dvw.reshape(rows, half).at[positions].add(own_grad[:, half:])
    dk_tok, dv_tok = to_token_layout([dk.astype(jnp.bfloat16), dv.astype(jnp.bfloat16)], core)
    return att_tok, dq_tok, dk_tok, dv_tok


def solution(mesh):
    seq_size, head_size = mesh.devices.shape
    split = Mesh(mesh.devices.reshape(seq_size, head_size // 2, 2), ("seq", "hx", "hc"))
    tok = P(("seq", "hx", "hc"), None)
    return jax.shard_map(
        body,
        mesh=split,
        in_specs=(tok, tok, tok, tok, P("seq", None)),
        out_specs=(tok, tok, tok, tok),
        check_vma=False,
    )
```

```python
import math

import jax
import jax.numpy as jnp
from jax import lax
from jax.sharding import Mesh
from jax.sharding import PartitionSpec as P

HEAD_DIM = 128
BLOCK = 128
SUMMARY = 8

MASKED_SCORE = -1e30
GROUP = ("seq", "hx")


def group_size():
    return lax.axis_size("seq") * lax.axis_size("hx")


def group_bits():
    size = group_size()
    bits = size.bit_length() - 1
    assert 1 << bits == size
    return bits


def exchange(x, mask):
    size = group_size()
    return lax.ppermute(x, GROUP, [(i, i ^ mask) for i in range(size)])


def gather_blocks(x):
    me = lax.axis_index("seq") * lax.axis_size("hx") + lax.axis_index("hx")
    held = x[None]
    for bit in reversed(range(group_bits())):
        got = exchange(held, 1 << bit)
        low = ((me >> bit) & 1) == 0
        held = jnp.where(low, jnp.stack([held, got], 1), jnp.stack([got, held], 1))
        held = held.reshape((-1,) + x.shape)
    return held.reshape((-1,) + x.shape[1:])


def reduce_blocks(x):
    me = lax.axis_index("seq") * lax.axis_size("hx") + lax.axis_index("hx")
    size = group_size()
    held = x.reshape((size, -1) + x.shape[1:])
    for bit in range(group_bits()):
        pairs = held.reshape((held.shape[0] // 2, 2) + held.shape[1:])
        mine = (me >> bit) & 1
        keep = jnp.where(mine == 0, pairs[:, 0], pairs[:, 1])
        send = jnp.where(mine == 0, pairs[:, 1], pairs[:, 0])
        held = keep + exchange(send, 1 << bit)
    return held.reshape(x.shape[0] // size, *x.shape[1:])


def swap_with_partner(x):
    return lax.ppermute(x, "hc", [(0, 1), (1, 0)])


def to_block_layout(arrays, core):
    rows, feats = arrays[0].shape
    half = feats // 2
    mine = [lax.dynamic_slice_in_dim(a, core * half, half, 1) for a in arrays]
    theirs = [lax.dynamic_slice_in_dim(a, (1 - core) * half, half, 1) for a in arrays]
    got = swap_with_partner(jnp.concatenate(theirs, axis=1))
    out = []
    for i, m in enumerate(mine):
        r = got[:, i * half:(i + 1) * half]
        out.append(jnp.where(core == 0, jnp.concatenate([m, r], 0), jnp.concatenate([r, m], 0)))
    return out


def to_token_layout(arrays, core):
    rows2, half = arrays[0].shape
    rows = rows2 // 2
    mine = [lax.dynamic_slice_in_dim(a, core * rows, rows, 0) for a in arrays]
    theirs = [lax.dynamic_slice_in_dim(a, (1 - core) * rows, rows, 0) for a in arrays]
    got = swap_with_partner(jnp.concatenate(theirs, axis=1))
    out = []
    for i, m in enumerate(mine):
        r = got[:, i * half:(i + 1) * half]
        out.append(jnp.where(core == 0, jnp.concatenate([m, r], 1), jnp.concatenate([r, m], 1)))
    return out


def body(queries, key_rows, value_rows, out_grad, summary_columns):
    core = lax.axis_index("hc")
    hx = lax.axis_index("hx")
    shard = lax.axis_index("seq")
    score_scale = 1.0 / math.sqrt(HEAD_DIM)
    f32 = jnp.float32

    qb, kb, vb, gb = to_block_layout([queries, key_rows, value_rows, out_grad], core)
    rows, half = qb.shape
    heads = half // HEAD_DIM
    nb = rows // BLOCK
    pair_count = summary_columns.shape[0] // nb
    first_block = (shard * pair_count + hx) * nb
    cols = lax.dynamic_slice_in_dim(summary_columns, hx * nb, nb, 0)
    positions = (jnp.arange(nb, dtype=jnp.int32)[:, None] * BLOCK + cols).reshape(-1)

    own_sum = jnp.concatenate([jnp.take(kb, positions, axis=0), jnp.take(vb, positions, axis=0)], axis=1)
    all_sum = gather_blocks(own_sum)
    sum_count = all_sum.shape[0]
    sk = all_sum[:, :half].reshape(sum_count, heads, HEAD_DIM)
    sv = all_sum[:, half:].reshape(sum_count, heads, HEAD_DIM)

    q = qb.reshape(nb, BLOCK, heads, HEAD_DIM)
    k = kb.reshape(nb, BLOCK, heads, HEAD_DIM)
    v = vb.reshape(nb, BLOCK, heads, HEAD_DIM)
    g = gb.reshape(nb, BLOCK, heads, HEAD_DIM)

    span = jnp.arange(BLOCK, dtype=jnp.int32)
    causal = (span[:, None] >= span[None, :])[None, None]
    key_block = jnp.arange(sum_count, dtype=jnp.int32) // SUMMARY
    query_block = first_block + jnp.arange(nb, dtype=jnp.int32)
    allowed = (key_block[None, :] < query_block[:, None])[:, None, None, :]

    sw = jnp.einsum("bqhd,bkhd->bhqk", q, k, preferred_element_type=f32) * score_scale
    ss = jnp.einsum("bqhd,khd->bhqk", q, sk, preferred_element_type=f32) * score_scale
    sw = jnp.where(causal, sw, MASKED_SCORE)
    ss = jnp.where(allowed, ss, MASKED_SCORE)
    top = jnp.maximum(jnp.max(sw, axis=3), jnp.max(ss, axis=3))
    ew = jnp.where(causal, jnp.exp(sw - top[..., None]), 0.0)
    es = jnp.where(allowed, jnp.exp(ss - top[..., None]), 0.0)
    log_norm = top + jnp.log(jnp.sum(ew, axis=3) + jnp.sum(es, axis=3))
    pw = jnp.where(causal, jnp.exp(sw - log_norm[..., None]), 0.0)
    ps = jnp.where(allowed, jnp.exp(ss - log_norm[..., None]), 0.0)
    pw_low = pw.astype(jnp.bfloat16)
    ps_low = ps.astype(jnp.bfloat16)
    att = jnp.einsum("bhqk,bkhd->bqhd", pw_low, v, preferred_element_type=f32) + jnp.einsum(
        "bhqk,khd->bqhd", ps_low, sv, preferred_element_type=f32
    )
    attended = att.astype(jnp.bfloat16)
    delta = jnp.einsum("bqhd,bqhd->bhq", g.astype(f32), attended.astype(f32), precision=lax.Precision.HIGHEST)

    dpw = jnp.einsum("bqhd,bkhd->bhqk", g, v, preferred_element_type=f32)
    dps = jnp.einsum("bqhd,khd->bhqk", g, sv, preferred_element_type=f32)
    dsw = (pw * (dpw - delta[..., None])).astype(jnp.bfloat16)
    dss = (ps * (dps - delta[..., None])).astype(jnp.bfloat16)
    dq = (
        jnp.einsum("bhqk,bkhd->bqhd", dsw, k, preferred_element_type=f32)
        + jnp.einsum("bhqk,khd->bqhd", dss, sk, preferred_element_type=f32)
    ) * score_scale
    dkw = jnp.einsum("bhqk,bqhd->bkhd", dsw, q, preferred_element_type=f32) * score_scale
    dvw = jnp.einsum("bhqk,bqhd->bkhd", pw_low, g, preferred_element_type=f32)
    dks = jnp.einsum("bhqk,bqhd->khd", dss, q, preferred_element_type=f32) * score_scale
    dvs = jnp.einsum("bhqk,bqhd->khd", ps_low, g, preferred_element_type=f32)

    att_tok, dq_tok = to_token_layout(
        [attended.reshape(rows, half), dq.astype(jnp.bfloat16).reshape(rows, half)], core
    )

    parts = jnp.concatenate([dks.reshape(sum_count, half), dvs.reshape(sum_count, half)], axis=1)
    own_grad = reduce_blocks(parts)
    dk = dkw.reshape(rows, half).at[positions].add(own_grad[:, :half])
    dv = dvw.reshape(rows, half).at[positions].add(own_grad[:, half:])
    dk_tok, dv_tok = to_token_layout([dk.astype(jnp.bfloat16), dv.astype(jnp.bfloat16)], core)
    return att_tok, dq_tok, dk_tok, dv_tok


def solution(mesh):
    seq_size, head_size = mesh.devices.shape
    split = Mesh(mesh.devices.reshape(seq_size, head_size // 2, 2), ("seq", "hx", "hc"))
    tok = P(("seq", "hx", "hc"), None)
    return jax.shard_map(
        body,
        mesh=split,
        in_specs=(tok, tok, tok, tok, P("seq", None)),
        out_specs=(tok, tok, tok, tok),
        check_vma=False,
    )
```

```python
import math

import jax
import jax.numpy as jnp
from jax import lax
from jax.sharding import Mesh
from jax.sharding import PartitionSpec as P

HEAD_DIM = 128
BLOCK = 128
SUMMARY = 8

MASKED_SCORE = -1e30
GROUP = ("seq", "hx")


def group_size():
    return lax.axis_size("seq") * lax.axis_size("hx")


def send_forward(x):
    size = group_size()
    got = [x]
    for d in range(1, size):
        got.append(lax.ppermute(x, GROUP, [(i, i + d) for i in range(size - d)]))
    return jnp.stack(got)


def send_back(parts):
    size = group_size()
    total = parts[0]
    for d in range(1, size):
        total = total + lax.ppermute(parts[d], GROUP, [(i, i - d) for i in range(d, size)])
    return total


def swap_with_partner(x):
    return lax.ppermute(x, "hc", [(0, 1), (1, 0)])


def to_block_layout(arrays, core):
    rows, feats = arrays[0].shape
    half = feats // 2
    mine = [lax.dynamic_slice_in_dim(a, core * half, half, 1) for a in arrays]
    theirs = [lax.dynamic_slice_in_dim(a, (1 - core) * half, half, 1) for a in arrays]
    got = swap_with_partner(jnp.concatenate(theirs, axis=1))
    out = []
    for i, m in enumerate(mine):
        r = got[:, i * half:(i + 1) * half]
        out.append(jnp.where(core == 0, jnp.concatenate([m, r], 0), jnp.concatenate([r, m], 0)))
    return out


def to_token_layout(arrays, core):
    rows2, half = arrays[0].shape
    rows = rows2 // 2
    mine = [lax.dynamic_slice_in_dim(a, core * rows, rows, 0) for a in arrays]
    theirs = [lax.dynamic_slice_in_dim(a, (1 - core) * rows, rows, 0) for a in arrays]
    got = swap_with_partner(jnp.concatenate(theirs, axis=1))
    out = []
    for i, m in enumerate(mine):
        r = got[:, i * half:(i + 1) * half]
        out.append(jnp.where(core == 0, jnp.concatenate([m, r], 1), jnp.concatenate([r, m], 1)))
    return out


def body(queries, key_rows, value_rows, out_grad, summary_columns):
    core = lax.axis_index("hc")
    hx = lax.axis_index("hx")
    shard = lax.axis_index("seq")
    score_scale = 1.0 / math.sqrt(HEAD_DIM)
    f32 = jnp.float32

    qb, kb, vb, gb = to_block_layout([queries, key_rows, value_rows, out_grad], core)
    rows, half = qb.shape
    heads = half // HEAD_DIM
    nb = rows // BLOCK
    pair_count = summary_columns.shape[0] // nb
    first_block = (shard * pair_count + hx) * nb
    cols = lax.dynamic_slice_in_dim(summary_columns, hx * nb, nb, 0)
    positions = (jnp.arange(nb, dtype=jnp.int32)[:, None] * BLOCK + cols).reshape(-1)

    own_sum = jnp.concatenate([jnp.take(kb, positions, axis=0), jnp.take(vb, positions, axis=0)], axis=1)
    me = shard * pair_count + hx
    all_sum = send_forward(own_sum)
    size = all_sum.shape[0]
    all_sum = all_sum.reshape(-1, all_sum.shape[-1])
    sum_count = all_sum.shape[0]
    sk = all_sum[:, :half].reshape(sum_count, heads, HEAD_DIM)
    sv = all_sum[:, half:].reshape(sum_count, heads, HEAD_DIM)

    q = qb.reshape(nb, BLOCK, heads, HEAD_DIM)
    k = kb.reshape(nb, BLOCK, heads, HEAD_DIM)
    v = vb.reshape(nb, BLOCK, heads, HEAD_DIM)
    g = gb.reshape(nb, BLOCK, heads, HEAD_DIM)

    span = jnp.arange(BLOCK, dtype=jnp.int32)
    causal = (span[:, None] >= span[None, :])[None, None]
    slot = jnp.arange(sum_count, dtype=jnp.int32) // SUMMARY
    key_block = (me - slot // nb) * nb + slot % nb
    query_block = first_block + jnp.arange(nb, dtype=jnp.int32)
    present = key_block >= 0
    allowed = (present[None, :] & (key_block[None, :] < query_block[:, None]))[:, None, None, :]

    sw = jnp.einsum("bqhd,bkhd->bhqk", q, k, preferred_element_type=f32) * score_scale
    ss = jnp.einsum("bqhd,khd->bhqk", q, sk, preferred_element_type=f32) * score_scale
    sw = jnp.where(causal, sw, MASKED_SCORE)
    ss = jnp.where(allowed, ss, MASKED_SCORE)
    top = jnp.maximum(jnp.max(sw, axis=3), jnp.max(ss, axis=3))
    ew = jnp.where(causal, jnp.exp(sw - top[..., None]), 0.0)
    es = jnp.where(allowed, jnp.exp(ss - top[..., None]), 0.0)
    log_norm = top + jnp.log(jnp.sum(ew, axis=3) + jnp.sum(es, axis=3))
    pw = jnp.where(causal, jnp.exp(sw - log_norm[..., None]), 0.0)
    ps = jnp.where(allowed, jnp.exp(ss - log_norm[..., None]), 0.0)
    pw_low = pw.astype(jnp.bfloat16)
    ps_low = ps.astype(jnp.bfloat16)
    att = jnp.einsum("bhqk,bkhd->bqhd", pw_low, v, preferred_element_type=f32) + jnp.einsum(
        "bhqk,khd->bqhd", ps_low, sv, preferred_element_type=f32
    )
    attended = att.astype(jnp.bfloat16)
    delta = jnp.einsum("bqhd,bqhd->bhq", g.astype(f32), attended.astype(f32), precision=lax.Precision.HIGHEST)

    dpw = jnp.einsum("bqhd,bkhd->bhqk", g, v, preferred_element_type=f32)
    dps = jnp.einsum("bqhd,khd->bhqk", g, sv, preferred_element_type=f32)
    dsw = (pw * (dpw - delta[..., None])).astype(jnp.bfloat16)
    dss = (ps * (dps - delta[..., None])).astype(jnp.bfloat16)
    dq = (
        jnp.einsum("bhqk,bkhd->bqhd", dsw, k, preferred_element_type=f32)
        + jnp.einsum("bhqk,khd->bqhd", dss, sk, preferred_element_type=f32)
    ) * score_scale
    dkw = jnp.einsum("bhqk,bqhd->bkhd", dsw, q, preferred_element_type=f32) * score_scale
    dvw = jnp.einsum("bhqk,bqhd->bkhd", pw_low, g, preferred_element_type=f32)
    dks = jnp.einsum("bhqk,bqhd->khd", dss, q, preferred_element_type=f32) * score_scale
    dvs = jnp.einsum("bhqk,bqhd->khd", ps_low, g, preferred_element_type=f32)

    att_tok, dq_tok = to_token_layout(
        [attended.reshape(rows, half), dq.astype(jnp.bfloat16).reshape(rows, half)], core
    )

    parts = jnp.concatenate([dks.reshape(sum_count, half), dvs.reshape(sum_count, half)], axis=1)
    own_grad = send_back(parts.reshape(size, -1, parts.shape[-1]))
    dk = dkw.reshape(rows, half).at[positions].add(own_grad[:, :half])
    dv = dvw.reshape(rows, half).at[positions].add(own_grad[:, half:])
    dk_tok, dv_tok = to_token_layout([dk.astype(jnp.bfloat16), dv.astype(jnp.bfloat16)], core)
    return att_tok, dq_tok, dk_tok, dv_tok


def solution(mesh):
    seq_size, head_size = mesh.devices.shape
    split = Mesh(mesh.devices.reshape(seq_size, head_size // 2, 2), ("seq", "hx", "hc"))
    tok = P(("seq", "hx", "hc"), None)
    return jax.shard_map(
        body,
        mesh=split,
        in_specs=(tok, tok, tok, tok, P("seq", None)),
        out_specs=(tok, tok, tok, tok),
        check_vma=False,
    )
```

```python
import math

import jax
import jax.numpy as jnp
from jax import lax
from jax.sharding import Mesh
from jax.sharding import PartitionSpec as P

HEAD_DIM = 128
BLOCK = 128
SUMMARY = 8

MASKED_SCORE = -1e30
GROUP = ("seq", "hx")


def group_size():
    return lax.axis_size("seq") * lax.axis_size("hx")


def group_bits():
    size = group_size()
    bits = size.bit_length() - 1
    assert 1 << bits == size
    return bits


def physical_bit(core, bit):
    if core == 1 and group_bits() >= 2 and bit < 2:
        return 1 - bit
    return bit


def exchange(x, bit):
    size = group_size()
    pairs = [
        (g * 2 + c, (g ^ (1 << physical_bit(c, bit))) * 2 + c) for g in range(size) for c in range(2)
    ]
    return lax.ppermute(x, ("seq", "hx", "hc"), pairs)


def swap_low_bits(x, core):
    if group_bits() < 2:
        return x
    size = x.shape[0]
    swapped = jnp.swapaxes(x.reshape((size // 4, 2, 2) + x.shape[1:]), 1, 2).reshape(x.shape)
    return jnp.where(core == 1, swapped, x)


def virtual_index(core):
    g = lax.axis_index("seq") * lax.axis_size("hx") + lax.axis_index("hx")
    if group_bits() < 2:
        return g
    swapped = (g & ~3) | ((g & 1) << 1) | ((g >> 1) & 1)
    return jnp.where(core == 1, swapped, g)


def gather_blocks(x, core):
    me = virtual_index(core)
    held = x[None]
    for bit in reversed(range(group_bits())):
        got = exchange(held, bit)
        low = ((me >> bit) & 1) == 0
        held = jnp.where(low, jnp.stack([held, got], 1), jnp.stack([got, held], 1))
        held = held.reshape((-1,) + x.shape)
    held = swap_low_bits(held, core)
    return held.reshape((-1,) + x.shape[1:])


def reduce_blocks(x, core):
    me = virtual_index(core)
    size = group_size()
    held = swap_low_bits(x.reshape((size, -1) + x.shape[1:]), core)
    for bit in range(group_bits()):
        pairs = held.reshape((held.shape[0] // 2, 2) + held.shape[1:])
        mine = (me >> bit) & 1
        keep = jnp.where(mine == 0, pairs[:, 0], pairs[:, 1])
        send = jnp.where(mine == 0, pairs[:, 1], pairs[:, 0])
        held = keep + exchange(send.astype(jnp.bfloat16), bit).astype(jnp.float32)
    return held.reshape(x.shape[0] // size, *x.shape[1:])


def swap_with_partner(x):
    return lax.ppermute(x, "hc", [(0, 1), (1, 0)])


def to_block_layout(arrays, core):
    rows, feats = arrays[0].shape
    half = feats // 2
    mine = [lax.dynamic_slice_in_dim(a, core * half, half, 1) for a in arrays]
    theirs = [lax.dynamic_slice_in_dim(a, (1 - core) * half, half, 1) for a in arrays]
    got = swap_with_partner(jnp.concatenate(theirs, axis=1))
    out = []
    for i, m in enumerate(mine):
        r = got[:, i * half:(i + 1) * half]
        out.append(jnp.where(core == 0, jnp.concatenate([m, r], 0), jnp.concatenate([r, m], 0)))
    return out


def to_token_layout(arrays, core):
    rows2, half = arrays[0].shape
    rows = rows2 // 2
    mine = [lax.dynamic_slice_in_dim(a, core * rows, rows, 0) for a in arrays]
    theirs = [lax.dynamic_slice_in_dim(a, (1 - core) * rows, rows, 0) for a in arrays]
    got = swap_with_partner(jnp.concatenate(theirs, axis=1))
    out = []
    for i, m in enumerate(mine):
        r = got[:, i * half:(i + 1) * half]
        out.append(jnp.where(core == 0, jnp.concatenate([m, r], 1), jnp.concatenate([r, m], 1)))
    return out


def body(queries, key_rows, value_rows, out_grad, summary_columns):
    core = lax.axis_index("hc")
    hx = lax.axis_index("hx")
    shard = lax.axis_index("seq")
    score_scale = 1.0 / math.sqrt(HEAD_DIM)
    f32 = jnp.float32

    qb, kb, vb, gb = to_block_layout([queries, key_rows, value_rows, out_grad], core)
    rows, half = qb.shape
    heads = half // HEAD_DIM
    nb = rows // BLOCK
    pair_count = summary_columns.shape[0] // nb
    first_block = (shard * pair_count + hx) * nb
    cols = lax.dynamic_slice_in_dim(summary_columns, hx * nb, nb, 0)
    positions = (jnp.arange(nb, dtype=jnp.int32)[:, None] * BLOCK + cols).reshape(-1)

    own_sum = jnp.concatenate([jnp.take(kb, positions, axis=0), jnp.take(vb, positions, axis=0)], axis=1)
    all_sum = gather_blocks(own_sum, core)
    sum_count = all_sum.shape[0]
    sk = all_sum[:, :half].reshape(sum_count, heads, HEAD_DIM)
    sv = all_sum[:, half:].reshape(sum_count, heads, HEAD_DIM)

    q = qb.reshape(nb, BLOCK, heads, HEAD_DIM)
    k = kb.reshape(nb, BLOCK, heads, HEAD_DIM)
    v = vb.reshape(nb, BLOCK, heads, HEAD_DIM)
    g = gb.reshape(nb, BLOCK, heads, HEAD_DIM)

    span = jnp.arange(BLOCK, dtype=jnp.int32)
    causal = (span[:, None] >= span[None, :])[None, None]
    key_block = jnp.arange(sum_count, dtype=jnp.int32) // SUMMARY
    query_block = first_block + jnp.arange(nb, dtype=jnp.int32)
    allowed = (key_block[None, :] < query_block[:, None])[:, None, None, :]

    sw = jnp.einsum("bqhd,bkhd->bhqk", q, k, preferred_element_type=f32) * score_scale
    ss = jnp.einsum("bqhd,khd->bhqk", q, sk, preferred_element_type=f32) * score_scale
    sw = jnp.where(causal, sw, MASKED_SCORE)
    ss = jnp.where(allowed, ss, MASKED_SCORE)
    top = jnp.maximum(jnp.max(sw, axis=3), jnp.max(ss, axis=3))
    ew = jnp.where(causal, jnp.exp(sw - top[..., None]), 0.0)
    es = jnp.where(allowed, jnp.exp(ss - top[..., None]), 0.0)
    log_norm = top + jnp.log(jnp.sum(ew, axis=3) + jnp.sum(es, axis=3))
    pw = jnp.where(causal, jnp.exp(sw - log_norm[..., None]), 0.0)
    ps = jnp.where(allowed, jnp.exp(ss - log_norm[..., None]), 0.0)
    pw_low = pw.astype(jnp.bfloat16)
    ps_low = ps.astype(jnp.bfloat16)
    att = jnp.einsum("bhqk,bkhd->bqhd", pw_low, v, preferred_element_type=f32) + jnp.einsum(
        "bhqk,khd->bqhd", ps_low, sv, preferred_element_type=f32
    )
    attended = att.astype(jnp.bfloat16)
    delta = jnp.einsum("bqhd,bqhd->bhq", g.astype(f32), attended.astype(f32), precision=lax.Precision.HIGHEST)

    dpw = jnp.einsum("bqhd,bkhd->bhqk", g, v, preferred_element_type=f32)
    dps = jnp.einsum("bqhd,khd->bhqk", g, sv, preferred_element_type=f32)
    dsw = (pw * (dpw - delta[..., None])).astype(jnp.bfloat16)
    dss = (ps * (dps - delta[..., None])).astype(jnp.bfloat16)
    dq = (
        jnp.einsum("bhqk,bkhd->bqhd", dsw, k, preferred_element_type=f32)
        + jnp.einsum("bhqk,khd->bqhd", dss, sk, preferred_element_type=f32)
    ) * score_scale
    dkw = jnp.einsum("bhqk,bqhd->bkhd", dsw, q, preferred_element_type=f32) * score_scale
    dvw = jnp.einsum("bhqk,bqhd->bkhd", pw_low, g, preferred_element_type=f32)
    dks = jnp.einsum("bhqk,bqhd->khd", dss, q, preferred_element_type=f32) * score_scale
    dvs = jnp.einsum("bhqk,bqhd->khd", ps_low, g, preferred_element_type=f32)

    att_tok, dq_tok = to_token_layout(
        [attended.reshape(rows, half), dq.astype(jnp.bfloat16).reshape(rows, half)], core
    )

    parts = jnp.concatenate([dks.reshape(sum_count, half), dvs.reshape(sum_count, half)], axis=1)
    own_grad = reduce_blocks(parts, core)
    dk = dkw.reshape(rows, half).at[positions].add(own_grad[:, :half])
    dv = dvw.reshape(rows, half).at[positions].add(own_grad[:, half:])
    dk_tok, dv_tok = to_token_layout([dk.astype(jnp.bfloat16), dv.astype(jnp.bfloat16)], core)
    return att_tok, dq_tok, dk_tok, dv_tok


def solution(mesh):
    seq_size, head_size = mesh.devices.shape
    split = Mesh(mesh.devices.reshape(seq_size, head_size // 2, 2), ("seq", "hx", "hc"))
    tok = P(("seq", "hx", "hc"), None)
    return jax.shard_map(
        body,
        mesh=split,
        in_specs=(tok, tok, tok, tok, P("seq", None)),
        out_specs=(tok, tok, tok, tok),
        check_vma=False,
    )
```

```python
import math

import jax
import jax.numpy as jnp
from jax import lax
from jax.experimental import pallas as pl
from jax.experimental.pallas import tpu as pltpu
from jax.sharding import Mesh
from jax.sharding import PartitionSpec as P

HEAD_DIM = 128
BLOCK = 128
SUMMARY = 8

MASKED_SCORE = -1e30
GROUP = ("seq", "hx")


def group_size():
    return lax.axis_size("seq") * lax.axis_size("hx")


def group_bits():
    size = group_size()
    bits = size.bit_length() - 1
    assert 1 << bits == size
    return bits


def physical_bit(core, bit):
    if core == 1 and group_bits() >= 2 and bit < 2:
        return 1 - bit
    return bit


def exchange(x, bit):
    size = group_size()
    pairs = [
        (g * 2 + c, (g ^ (1 << physical_bit(c, bit))) * 2 + c) for g in range(size) for c in range(2)
    ]
    return lax.ppermute(x, ("seq", "hx", "hc"), pairs)


def swap_low_bits(x, core):
    if group_bits() < 2:
        return x
    size = x.shape[0]
    swapped = jnp.swapaxes(x.reshape((size // 4, 2, 2) + x.shape[1:]), 1, 2).reshape(x.shape)
    return jnp.where(core == 1, swapped, x)


def virtual_index(core):
    g = lax.axis_index("seq") * lax.axis_size("hx") + lax.axis_index("hx")
    if group_bits() < 2:
        return g
    swapped = (g & ~3) | ((g & 1) << 1) | ((g >> 1) & 1)
    return jnp.where(core == 1, swapped, g)


def gather_blocks(x, core):
    me = virtual_index(core)
    held = x[None]
    for bit in reversed(range(group_bits())):
        got = exchange(held, bit)
        low = ((me >> bit) & 1) == 0
        held = jnp.where(low, jnp.stack([held, got], 1), jnp.stack([got, held], 1))
        held = held.reshape((-1,) + x.shape)
    held = swap_low_bits(held, core)
    return held.reshape((-1,) + x.shape[1:])


def reduce_blocks(x, core):
    me = virtual_index(core)
    size = group_size()
    held = swap_low_bits(x.reshape((size, -1) + x.shape[1:]), core)
    for bit in range(group_bits()):
        pairs = held.reshape((held.shape[0] // 2, 2) + held.shape[1:])
        mine = (me >> bit) & 1
        keep = jnp.where(mine == 0, pairs[:, 0], pairs[:, 1])
        send = jnp.where(mine == 0, pairs[:, 1], pairs[:, 0])
        held = keep + exchange(send.astype(jnp.bfloat16), bit).astype(jnp.float32)
    return held.reshape(x.shape[0] // size, *x.shape[1:])


def swap_with_partner(x):
    return lax.ppermute(x, "hc", [(0, 1), (1, 0)])


def to_block_layout(arrays, core):
    rows, feats = arrays[0].shape
    half = feats // 2
    mine = [lax.dynamic_slice_in_dim(a, core * half, half, 1) for a in arrays]
    theirs = [lax.dynamic_slice_in_dim(a, (1 - core) * half, half, 1) for a in arrays]
    got = swap_with_partner(jnp.concatenate(theirs, axis=1))
    out = []
    for i, m in enumerate(mine):
        r = got[:, i * half:(i + 1) * half]
        out.append(jnp.where(core == 0, jnp.concatenate([m, r], 0), jnp.concatenate([r, m], 0)))
    return out


def to_token_layout(arrays, core):
    rows2, half = arrays[0].shape
    rows = rows2 // 2
    mine = [lax.dynamic_slice_in_dim(a, core * rows, rows, 0) for a in arrays]
    theirs = [lax.dynamic_slice_in_dim(a, (1 - core) * rows, rows, 0) for a in arrays]
    got = swap_with_partner(jnp.concatenate(theirs, axis=1))
    out = []
    for i, m in enumerate(mine):
        r = got[:, i * half:(i + 1) * half]
        out.append(jnp.where(core == 0, jnp.concatenate([m, r], 1), jnp.concatenate([r, m], 1)))
    return out


def mm(a, b, trans_a=False, trans_b=False):
    dims = (((0 if trans_a else 1,), (1 if trans_b else 0,)), ((), ()))
    return lax.dot_general(a, b, dims, preferred_element_type=jnp.float32)


def attention_kernel(
    q_ref, k_ref, v_ref, g_ref, s_ref, mask_ref, att_ref, dq_ref, dkw_ref, dvw_ref, ds_ref
):
    j = pl.program_id(1)
    scale = 1.0 / math.sqrt(HEAD_DIM)
    f32 = jnp.float32
    bf16 = jnp.bfloat16
    q = q_ref[...]
    k = k_ref[...]
    v = v_ref[...]
    g = g_ref[...]
    sk = s_ref[:, :HEAD_DIM]
    sv = s_ref[:, HEAD_DIM:]
    allowed = mask_ref[0:1, :] > 0
    row = lax.broadcasted_iota(jnp.int32, (BLOCK, BLOCK), 0)
    col = lax.broadcasted_iota(jnp.int32, (BLOCK, BLOCK), 1)
    causal = row >= col

    sw = jnp.where(causal, mm(q, k, trans_b=True) * scale, MASKED_SCORE)
    ss = jnp.where(allowed, mm(q, sk, trans_b=True) * scale, MASKED_SCORE)
    top = jnp.maximum(jnp.max(sw, axis=1, keepdims=True), jnp.max(ss, axis=1, keepdims=True))
    total = jnp.sum(jnp.exp(sw - top), axis=1, keepdims=True) + jnp.sum(
        jnp.exp(ss - top), axis=1, keepdims=True
    )
    log_norm = top + jnp.log(total)
    pw = jnp.where(causal, jnp.exp(sw - log_norm), 0.0)
    ps = jnp.where(allowed, jnp.exp(ss - log_norm), 0.0)
    pw_low = pw.astype(bf16)
    ps_low = ps.astype(bf16)
    att = (mm(pw_low, v) + mm(ps_low, sv)).astype(bf16)
    att_ref[...] = att
    delta = jnp.sum(g.astype(f32) * att.astype(f32), axis=1, keepdims=True)
    dsw = (pw * (mm(g, v, trans_b=True) - delta)).astype(bf16)
    dss = (ps * (mm(g, sv, trans_b=True) - delta)).astype(bf16)
    dq_ref[...] = ((mm(dsw, k) + mm(dss, sk)) * scale).astype(bf16)
    dkw_ref[...] = mm(dsw, q, trans_a=True) * scale
    dvw_ref[...] = mm(pw_low, g, trans_a=True)
    dks = mm(dss, q, trans_a=True) * scale
    dvs = mm(ps_low, g, trans_a=True)

    @pl.when(j == 0)
    def _():
        ds_ref[:, :HEAD_DIM] = dks
        ds_ref[:, HEAD_DIM:] = dvs

    @pl.when(j > 0)
    def _():
        ds_ref[:, :HEAD_DIM] += dks
        ds_ref[:, HEAD_DIM:] += dvs


def attention(q, k, v, g, summary, mask):
    rows, half = q.shape
    heads = half // HEAD_DIM
    nb = rows // BLOCK
    count = summary.shape[0]
    tile = pl.BlockSpec((BLOCK, HEAD_DIM), lambda h, j: (j, h))
    pair = pl.BlockSpec((count, 2 * HEAD_DIM), lambda h, j: (0, h))
    bf16 = jnp.bfloat16
    f32 = jnp.float32
    flops = 2 * rows * heads * HEAD_DIM * (BLOCK + count) * 6
    return pl.pallas_call(
        attention_kernel,
        grid=(heads, nb),
        in_specs=[tile, tile, tile, tile, pair, pl.BlockSpec((8, count), lambda h, j: (j, 0))],
        out_specs=[tile, tile, tile, tile, pair],
        out_shape=[
            jax.ShapeDtypeStruct((rows, half), bf16),
            jax.ShapeDtypeStruct((rows, half), bf16),
            jax.ShapeDtypeStruct((rows, half), f32),
            jax.ShapeDtypeStruct((rows, half), f32),
            jax.ShapeDtypeStruct((count, 2 * half), f32),
        ],
        cost_estimate=pl.CostEstimate(
            flops=flops, transcendentals=rows * heads * (BLOCK + count) * 2,
            bytes_accessed=rows * half * 2 * 8 + count * half * 2 * 6,
        ),
    )(q, k, v, g, summary, mask)


def body(queries, key_rows, value_rows, out_grad, summary_columns):
    core = lax.axis_index("hc")
    hx = lax.axis_index("hx")
    shard = lax.axis_index("seq")
    score_scale = 1.0 / math.sqrt(HEAD_DIM)
    f32 = jnp.float32

    qb, kb, vb, gb = to_block_layout([queries, key_rows, value_rows, out_grad], core)
    rows, half = qb.shape
    heads = half // HEAD_DIM
    nb = rows // BLOCK
    pair_count = summary_columns.shape[0] // nb
    first_block = (shard * pair_count + hx) * nb
    cols = lax.dynamic_slice_in_dim(summary_columns, hx * nb, nb, 0)
    positions = (jnp.arange(nb, dtype=jnp.int32)[:, None] * BLOCK + cols).reshape(-1)

    own_sum = jnp.stack(
        [
            jnp.take(kb, positions, axis=0).reshape(-1, heads, HEAD_DIM),
            jnp.take(vb, positions, axis=0).reshape(-1, heads, HEAD_DIM),
        ],
        axis=2,
    ).reshape(-1, 2 * half)
    all_sum = gather_blocks(own_sum, core)
    sum_count = all_sum.shape[0]
    key_block = jnp.arange(sum_count, dtype=jnp.int32) // SUMMARY
    query_block = first_block + jnp.arange(nb, dtype=jnp.int32)
    mask = (key_block[None, :] < query_block[:, None]).astype(jnp.int32)
    mask = jnp.repeat(mask, 8, axis=0)

    attended, dq, dkw, dvw, parts = attention(qb, kb, vb, gb, all_sum, mask)
    att_tok, dq_tok = to_token_layout([attended, dq], core)

    own_grad = reduce_blocks(parts, core).reshape(-1, heads, 2, HEAD_DIM)
    dk = dkw.at[positions].add(own_grad[:, :, 0].reshape(-1, half))
    dv = dvw.at[positions].add(own_grad[:, :, 1].reshape(-1, half))
    dk_tok, dv_tok = to_token_layout([dk.astype(jnp.bfloat16), dv.astype(jnp.bfloat16)], core)
    return att_tok, dq_tok, dk_tok, dv_tok


def solution(mesh):
    seq_size, head_size = mesh.devices.shape
    split = Mesh(mesh.devices.reshape(seq_size, head_size // 2, 2), ("seq", "hx", "hc"))
    tok = P(("seq", "hx", "hc"), None)
    return jax.shard_map(
        body,
        mesh=split,
        in_specs=(tok, tok, tok, tok, P("seq", None)),
        out_specs=(tok, tok, tok, tok),
        check_vma=False,
    )
```

```python
import math

import jax
import jax.numpy as jnp
from jax import lax
from jax.experimental import pallas as pl
from jax.experimental.pallas import tpu as pltpu
from jax.sharding import Mesh
from jax.sharding import PartitionSpec as P

HEAD_DIM = 128
BLOCK = 128
SUMMARY = 8

MASKED_SCORE = -1e30
GROUP = ("seq", "hx")


def group_size():
    return lax.axis_size("seq") * lax.axis_size("hx")


def group_bits():
    size = group_size()
    bits = size.bit_length() - 1
    assert 1 << bits == size
    return bits


def physical_bit(core, bit):
    if core == 1 and group_bits() >= 2 and bit < 2:
        return 1 - bit
    return bit


def exchange(x, bit):
    size = group_size()
    pairs = [
        (g * 2 + c, (g ^ (1 << physical_bit(c, bit))) * 2 + c) for g in range(size) for c in range(2)
    ]
    return lax.ppermute(x, ("seq", "hx", "hc"), pairs)


def swap_low_bits(x, core):
    if group_bits() < 2:
        return x
    size = x.shape[0]
    swapped = jnp.swapaxes(x.reshape((size // 4, 2, 2) + x.shape[1:]), 1, 2).reshape(x.shape)
    return jnp.where(core == 1, swapped, x)


def virtual_index(core):
    g = lax.axis_index("seq") * lax.axis_size("hx") + lax.axis_index("hx")
    if group_bits() < 2:
        return g
    swapped = (g & ~3) | ((g & 1) << 1) | ((g >> 1) & 1)
    return jnp.where(core == 1, swapped, g)


def gather_blocks(x, core):
    me = virtual_index(core)
    held = x[None]
    for bit in reversed(range(group_bits())):
        got = exchange(held, bit)
        low = ((me >> bit) & 1) == 0
        held = jnp.where(low, jnp.stack([held, got], 1), jnp.stack([got, held], 1))
        held = held.reshape((-1,) + x.shape)
    held = swap_low_bits(held, core)
    return held.reshape((-1,) + x.shape[1:])


def reduce_blocks(x, core):
    me = virtual_index(core)
    size = group_size()
    held = swap_low_bits(x.reshape((size, -1) + x.shape[1:]), core)
    for bit in range(group_bits()):
        pairs = held.reshape((held.shape[0] // 2, 2) + held.shape[1:])
        mine = (me >> bit) & 1
        keep = jnp.where(mine == 0, pairs[:, 0], pairs[:, 1])
        send = jnp.where(mine == 0, pairs[:, 1], pairs[:, 0])
        held = keep + exchange(send.astype(jnp.bfloat16), bit).astype(jnp.float32)
    return held.reshape(x.shape[0] // size, *x.shape[1:])


def swap_with_partner(x):
    return lax.ppermute(x, "hc", [(0, 1), (1, 0)])


def to_block_layout(arrays, core):
    rows, feats = arrays[0].shape
    half = feats // 2
    mine = [lax.dynamic_slice_in_dim(a, core * half, half, 1) for a in arrays]
    theirs = [lax.dynamic_slice_in_dim(a, (1 - core) * half, half, 1) for a in arrays]
    got = swap_with_partner(jnp.concatenate(theirs, axis=1))
    out = []
    for i, m in enumerate(mine):
        r = got[:, i * half:(i + 1) * half]
        out.append(jnp.where(core == 0, jnp.concatenate([m, r], 0), jnp.concatenate([r, m], 0)))
    return out


def to_token_layout(arrays, core):
    rows2, half = arrays[0].shape
    rows = rows2 // 2
    mine = [lax.dynamic_slice_in_dim(a, core * rows, rows, 0) for a in arrays]
    theirs = [lax.dynamic_slice_in_dim(a, (1 - core) * rows, rows, 0) for a in arrays]
    got = swap_with_partner(jnp.concatenate(theirs, axis=1))
    out = []
    for i, m in enumerate(mine):
        r = got[:, i * half:(i + 1) * half]
        out.append(jnp.where(core == 0, jnp.concatenate([m, r], 1), jnp.concatenate([r, m], 1)))
    return out


def mm(a, b, trans_a=False, trans_b=False):
    dims = (((0 if trans_a else 1,), (1 if trans_b else 0,)), ((), ()))
    return lax.dot_general(a, b, dims, preferred_element_type=jnp.float32)


def forward_kernel(q_ref, k_ref, v_ref, g_ref, s_ref, mask_ref, att_ref, stats_ref, dqs_ref, ds_ref):
    j = pl.program_id(1)
    scale = 1.0 / math.sqrt(HEAD_DIM)
    f32 = jnp.float32
    bf16 = jnp.bfloat16
    q = q_ref[...]
    k = k_ref[...]
    v = v_ref[...]
    g = g_ref[...]
    sk = s_ref[:, :HEAD_DIM]
    sv = s_ref[:, HEAD_DIM:]
    allowed = mask_ref[0:1, :] > 0
    row = lax.broadcasted_iota(jnp.int32, (BLOCK, BLOCK), 0)
    col = lax.broadcasted_iota(jnp.int32, (BLOCK, BLOCK), 1)
    causal = row >= col

    sw = jnp.where(causal, mm(q, k, trans_b=True) * scale, MASKED_SCORE)
    ss = jnp.where(allowed, mm(q, sk, trans_b=True) * scale, MASKED_SCORE)
    top = jnp.maximum(jnp.max(sw, axis=1, keepdims=True), jnp.max(ss, axis=1, keepdims=True))
    total = jnp.sum(jnp.exp(sw - top), axis=1, keepdims=True) + jnp.sum(
        jnp.exp(ss - top), axis=1, keepdims=True
    )
    log_norm = top + jnp.log(total)
    pw = jnp.where(causal, jnp.exp(sw - log_norm), 0.0)
    ps = jnp.where(allowed, jnp.exp(ss - log_norm), 0.0)
    ps_low = ps.astype(bf16)
    att = (mm(pw.astype(bf16), v) + mm(ps_low, sv)).astype(bf16)
    att_ref[...] = att
    delta = jnp.sum(g.astype(f32) * att.astype(f32), axis=1, keepdims=True)
    stats_ref[:, :HEAD_DIM] = jnp.broadcast_to(log_norm, (BLOCK, HEAD_DIM))
    stats_ref[:, HEAD_DIM:] = jnp.broadcast_to(delta, (BLOCK, HEAD_DIM))
    dss = (ps * (mm(g, sv, trans_b=True) - delta)).astype(bf16)
    dqs_ref[...] = mm(dss, sk) * scale
    dks = mm(dss, q, trans_a=True) * scale
    dvs = mm(ps_low, g, trans_a=True)

    @pl.when(j == 0)
    def _():
        ds_ref[:, :HEAD_DIM] = dks
        ds_ref[:, HEAD_DIM:] = dvs

    @pl.when(j > 0)
    def _():
        ds_ref[:, :HEAD_DIM] += dks
        ds_ref[:, HEAD_DIM:] += dvs


def window_kernel(q_ref, k_ref, v_ref, g_ref, stats_ref, dqs_ref, dq_ref, dkw_ref, dvw_ref):
    scale = 1.0 / math.sqrt(HEAD_DIM)
    bf16 = jnp.bfloat16
    q = q_ref[...]
    k = k_ref[...]
    v = v_ref[...]
    g = g_ref[...]
    log_norm = stats_ref[:, 0:1]
    delta = stats_ref[:, HEAD_DIM:HEAD_DIM + 1]
    row = lax.broadcasted_iota(jnp.int32, (BLOCK, BLOCK), 0)
    col = lax.broadcasted_iota(jnp.int32, (BLOCK, BLOCK), 1)
    causal = row >= col
    sw = mm(q, k, trans_b=True) * scale
    pw = jnp.where(causal, jnp.exp(jnp.where(causal, sw, MASKED_SCORE) - log_norm), 0.0)
    dsw = (pw * (mm(g, v, trans_b=True) - delta)).astype(bf16)
    dq_ref[...] = (mm(dsw, k) * scale + dqs_ref[...]).astype(bf16)
    dkw_ref[...] = mm(dsw, q, trans_a=True) * scale
    dvw_ref[...] = mm(pw.astype(bf16), g, trans_a=True)


def attention_forward(q, k, v, g, summary, mask):
    rows, half = q.shape
    heads = half // HEAD_DIM
    nb = rows // BLOCK
    count = summary.shape[0]
    tile = pl.BlockSpec((BLOCK, HEAD_DIM), lambda h, j: (j, h))
    wide = pl.BlockSpec((BLOCK, 2 * HEAD_DIM), lambda h, j: (j, h))
    pair = pl.BlockSpec((count, 2 * HEAD_DIM), lambda h, j: (0, h))
    f32 = jnp.float32
    return pl.pallas_call(
        forward_kernel,
        grid=(heads, nb),
        in_specs=[tile, tile, tile, tile, pair, pl.BlockSpec((8, count), lambda h, j: (j, 0))],
        out_specs=[tile, wide, tile, pair],
        out_shape=[
            jax.ShapeDtypeStruct((rows, half), jnp.bfloat16),
            jax.ShapeDtypeStruct((rows, 2 * half), f32),
            jax.ShapeDtypeStruct((rows, half), f32),
            jax.ShapeDtypeStruct((count, 2 * half), f32),
        ],
        cost_estimate=pl.CostEstimate(
            flops=2 * rows * half * (BLOCK * 2 + count * 5),
            transcendentals=rows * heads * (BLOCK + count) * 2,
            bytes_accessed=rows * half * 2 * 10 + count * half * 2 * 6,
        ),
    )(q, k, v, g, summary, mask)


def attention_window(q, k, v, g, stats, dq_summary):
    rows, half = q.shape
    heads = half // HEAD_DIM
    nb = rows // BLOCK
    tile = pl.BlockSpec((BLOCK, HEAD_DIM), lambda h, j: (j, h))
    wide = pl.BlockSpec((BLOCK, 2 * HEAD_DIM), lambda h, j: (j, h))
    f32 = jnp.float32
    return pl.pallas_call(
        window_kernel,
        grid=(heads, nb),
        in_specs=[tile, tile, tile, tile, wide, tile],
        out_specs=[tile, tile, tile],
        out_shape=[
            jax.ShapeDtypeStruct((rows, half), jnp.bfloat16),
            jax.ShapeDtypeStruct((rows, half), f32),
            jax.ShapeDtypeStruct((rows, half), f32),
        ],
        cost_estimate=pl.CostEstimate(
            flops=2 * rows * half * BLOCK * 5,
            transcendentals=rows * heads * BLOCK,
            bytes_accessed=rows * half * 2 * 14,
        ),
    )(q, k, v, g, stats, dq_summary)


def body(queries, key_rows, value_rows, out_grad, summary_columns):
    core = lax.axis_index("hc")
    hx = lax.axis_index("hx")
    shard = lax.axis_index("seq")
    score_scale = 1.0 / math.sqrt(HEAD_DIM)
    f32 = jnp.float32

    qb, kb, vb, gb = to_block_layout([queries, key_rows, value_rows, out_grad], core)
    rows, half = qb.shape
    heads = half // HEAD_DIM
    nb = rows // BLOCK
    pair_count = summary_columns.shape[0] // nb
    first_block = (shard * pair_count + hx) * nb
    cols = lax.dynamic_slice_in_dim(summary_columns, hx * nb, nb, 0)
    positions = (jnp.arange(nb, dtype=jnp.int32)[:, None] * BLOCK + cols).reshape(-1)

    own_sum = jnp.stack(
        [
            jnp.take(kb, positions, axis=0).reshape(-1, heads, HEAD_DIM),
            jnp.take(vb, positions, axis=0).reshape(-1, heads, HEAD_DIM),
        ],
        axis=2,
    ).reshape(-1, 2 * half)
    all_sum = gather_blocks(own_sum, core)
    sum_count = all_sum.shape[0]
    key_block = jnp.arange(sum_count, dtype=jnp.int32) // SUMMARY
    query_block = first_block + jnp.arange(nb, dtype=jnp.int32)
    mask = (key_block[None, :] < query_block[:, None]).astype(jnp.int32)
    mask = jnp.repeat(mask, 8, axis=0)

    attended, stats, dq_summary, parts = attention_forward(qb, kb, vb, gb, all_sum, mask)
    own_grad = reduce_blocks(parts, core).reshape(-1, heads, 2, HEAD_DIM)
    dq, dkw, dvw = attention_window(qb, kb, vb, gb, stats, dq_summary)
    att_tok, dq_tok = to_token_layout([attended, dq], core)

    dk = dkw.at[positions].add(own_grad[:, :, 0].reshape(-1, half))
    dv = dvw.at[positions].add(own_grad[:, :, 1].reshape(-1, half))
    dk_tok, dv_tok = to_token_layout([dk.astype(jnp.bfloat16), dv.astype(jnp.bfloat16)], core)
    return att_tok, dq_tok, dk_tok, dv_tok


def solution(mesh):
    seq_size, head_size = mesh.devices.shape
    split = Mesh(mesh.devices.reshape(seq_size, head_size // 2, 2), ("seq", "hx", "hc"))
    tok = P(("seq", "hx", "hc"), None)
    return jax.shard_map(
        body,
        mesh=split,
        in_specs=(tok, tok, tok, tok, P("seq", None)),
        out_specs=(tok, tok, tok, tok),
        check_vma=False,
    )
```

```python
import math

import jax
import jax.numpy as jnp
from jax import lax
from jax.experimental import pallas as pl
from jax.experimental.pallas import tpu as pltpu
from jax.sharding import Mesh
from jax.sharding import PartitionSpec as P

HEAD_DIM = 128
BLOCK = 128
SUMMARY = 8

MASKED_SCORE = -1e30
GROUP = ("seq", "hx")
HEADS_PER_STEP = 4


def group_size():
    return lax.axis_size("seq") * lax.axis_size("hx")


def group_bits():
    size = group_size()
    bits = size.bit_length() - 1
    assert 1 << bits == size
    return bits


def physical_bit(core, bit):
    if core == 1 and group_bits() >= 2 and bit < 2:
        return 1 - bit
    return bit


def exchange(x, bit):
    size = group_size()
    pairs = [
        (g * 2 + c, (g ^ (1 << physical_bit(c, bit))) * 2 + c) for g in range(size) for c in range(2)
    ]
    return lax.ppermute(x, ("seq", "hx", "hc"), pairs)


def swap_low_bits(x, core):
    if group_bits() < 2:
        return x
    size = x.shape[0]
    swapped = jnp.swapaxes(x.reshape((size // 4, 2, 2) + x.shape[1:]), 1, 2).reshape(x.shape)
    return jnp.where(core == 1, swapped, x)


def virtual_index(core):
    g = lax.axis_index("seq") * lax.axis_size("hx") + lax.axis_index("hx")
    if group_bits() < 2:
        return g
    swapped = (g & ~3) | ((g & 1) << 1) | ((g >> 1) & 1)
    return jnp.where(core == 1, swapped, g)


def gather_blocks(x, core):
    me = virtual_index(core)
    held = x[None]
    for bit in reversed(range(group_bits())):
        got = exchange(held, bit)
        low = ((me >> bit) & 1) == 0
        held = jnp.where(low, jnp.stack([held, got], 1), jnp.stack([got, held], 1))
        held = held.reshape((-1,) + x.shape)
    held = swap_low_bits(held, core)
    return held.reshape((-1,) + x.shape[1:])


def reduce_blocks(x, core):
    me = virtual_index(core)
    size = group_size()
    held = swap_low_bits(x.reshape((size, -1) + x.shape[1:]), core)
    for bit in range(group_bits()):
        pairs = held.reshape((held.shape[0] // 2, 2) + held.shape[1:])
        mine = (me >> bit) & 1
        keep = jnp.where(mine == 0, pairs[:, 0], pairs[:, 1])
        send = jnp.where(mine == 0, pairs[:, 1], pairs[:, 0])
        held = keep + exchange(send.astype(jnp.bfloat16), bit).astype(jnp.float32)
    return held.reshape(x.shape[0] // size, *x.shape[1:])


def swap_with_partner(x):
    return lax.ppermute(x, "hc", [(0, 1), (1, 0)])


def to_block_layout(arrays, core):
    rows, feats = arrays[0].shape
    half = feats // 2
    mine = [lax.dynamic_slice_in_dim(a, core * half, half, 1) for a in arrays]
    theirs = [lax.dynamic_slice_in_dim(a, (1 - core) * half, half, 1) for a in arrays]
    got = swap_with_partner(jnp.concatenate(theirs, axis=1))
    out = []
    for i, m in enumerate(mine):
        r = got[:, i * half:(i + 1) * half]
        out.append(jnp.where(core == 0, jnp.concatenate([m, r], 0), jnp.concatenate([r, m], 0)))
    return out


def to_token_layout(arrays, core):
    rows2, half = arrays[0].shape
    rows = rows2 // 2
    mine = [lax.dynamic_slice_in_dim(a, core * rows, rows, 0) for a in arrays]
    theirs = [lax.dynamic_slice_in_dim(a, (1 - core) * rows, rows, 0) for a in arrays]
    got = swap_with_partner(jnp.concatenate(theirs, axis=1))
    out = []
    for i, m in enumerate(mine):
        r = got[:, i * half:(i + 1) * half]
        out.append(jnp.where(core == 0, jnp.concatenate([m, r], 1), jnp.concatenate([r, m], 1)))
    return out


def mm(a, b, trans_a=False, trans_b=False):
    dims = (((0 if trans_a else 1,), (1 if trans_b else 0,)), ((), ()))
    return lax.dot_general(a, b, dims, preferred_element_type=jnp.float32)


def attention_kernel(
    q_all, k_all, v_all, g_all, s_all, mask_ref, att_all, dq_all, dkw_all, dvw_all, ds_all
):
    j = pl.program_id(1)
    scale = 1.0 / math.sqrt(HEAD_DIM)
    f32 = jnp.float32
    bf16 = jnp.bfloat16
    allowed = mask_ref[0:1, :] > 0
    row = lax.broadcasted_iota(jnp.int32, (BLOCK, BLOCK), 0)
    col = lax.broadcasted_iota(jnp.int32, (BLOCK, BLOCK), 1)
    causal = row >= col
    for hh in range(q_all.shape[1] // HEAD_DIM):
        cols = pl.ds(hh * HEAD_DIM, HEAD_DIM)
        q = q_all[:, cols]
        k = k_all[:, cols]
        v = v_all[:, cols]
        g = g_all[:, cols]
        sk = s_all[:, pl.ds(2 * hh * HEAD_DIM, HEAD_DIM)]
        sv = s_all[:, pl.ds((2 * hh + 1) * HEAD_DIM, HEAD_DIM)]

        sw = jnp.where(causal, mm(q, k, trans_b=True) * scale, MASKED_SCORE)
        ss = jnp.where(allowed, mm(q, sk, trans_b=True) * scale, MASKED_SCORE)
        top = jnp.maximum(jnp.max(sw, axis=1, keepdims=True), jnp.max(ss, axis=1, keepdims=True))
        total = jnp.sum(jnp.exp(sw - top), axis=1, keepdims=True) + jnp.sum(
            jnp.exp(ss - top), axis=1, keepdims=True
        )
        log_norm = top + jnp.log(total)
        pw = jnp.where(causal, jnp.exp(sw - log_norm), 0.0)
        ps = jnp.where(allowed, jnp.exp(ss - log_norm), 0.0)
        pw_low = pw.astype(bf16)
        ps_low = ps.astype(bf16)
        att = (mm(pw_low, v) + mm(ps_low, sv)).astype(bf16)
        att_all[:, cols] = att
        delta = jnp.sum(g.astype(f32) * att.astype(f32), axis=1, keepdims=True)
        dsw = (pw * (mm(g, v, trans_b=True) - delta)).astype(bf16)
        dss = (ps * (mm(g, sv, trans_b=True) - delta)).astype(bf16)
        dq_all[:, cols] = ((mm(dsw, k) + mm(dss, sk)) * scale).astype(bf16)
        dkw_all[:, cols] = mm(dsw, q, trans_a=True) * scale
        dvw_all[:, cols] = mm(pw_low, g, trans_a=True)
        dks = mm(dss, q, trans_a=True) * scale
        dvs = mm(ps_low, g, trans_a=True)
        kcols = pl.ds(2 * hh * HEAD_DIM, HEAD_DIM)
        vcols = pl.ds((2 * hh + 1) * HEAD_DIM, HEAD_DIM)

        @pl.when(j == 0)
        def _():
            ds_all[:, kcols] = dks
            ds_all[:, vcols] = dvs

        @pl.when(j > 0)
        def _():
            ds_all[:, kcols] += dks
            ds_all[:, vcols] += dvs


def attention(q, k, v, g, summary, mask):
    rows, half = q.shape
    heads = half // HEAD_DIM
    nb = rows // BLOCK
    count = summary.shape[0]
    per_step = math.gcd(heads, HEADS_PER_STEP)
    tile = pl.BlockSpec((BLOCK, per_step * HEAD_DIM), lambda h, j: (j, h))
    pair = pl.BlockSpec((count, 2 * per_step * HEAD_DIM), lambda h, j: (0, h))
    bf16 = jnp.bfloat16
    f32 = jnp.float32
    flops = 2 * rows * heads * HEAD_DIM * (BLOCK + count) * 6
    return pl.pallas_call(
        attention_kernel,
        grid=(heads // per_step, nb),
        in_specs=[tile, tile, tile, tile, pair, pl.BlockSpec((8, count), lambda h, j: (j, 0))],
        out_specs=[tile, tile, tile, tile, pair],
        out_shape=[
            jax.ShapeDtypeStruct((rows, half), bf16),
            jax.ShapeDtypeStruct((rows, half), bf16),
            jax.ShapeDtypeStruct((rows, half), f32),
            jax.ShapeDtypeStruct((rows, half), f32),
            jax.ShapeDtypeStruct((count, 2 * half), f32),
        ],
        cost_estimate=pl.CostEstimate(
            flops=flops, transcendentals=rows * heads * (BLOCK + count) * 2,
            bytes_accessed=rows * half * 2 * 8 + count * half * 2 * 6,
        ),
    )(q, k, v, g, summary, mask)


def body(queries, key_rows, value_rows, out_grad, summary_columns):
    core = lax.axis_index("hc")
    hx = lax.axis_index("hx")
    shard = lax.axis_index("seq")
    score_scale = 1.0 / math.sqrt(HEAD_DIM)
    f32 = jnp.float32

    qb, kb, vb, gb = to_block_layout([queries, key_rows, value_rows, out_grad], core)
    rows, half = qb.shape
    heads = half // HEAD_DIM
    nb = rows // BLOCK
    pair_count = summary_columns.shape[0] // nb
    first_block = (shard * pair_count + hx) * nb
    cols = lax.dynamic_slice_in_dim(summary_columns, hx * nb, nb, 0)
    positions = (jnp.arange(nb, dtype=jnp.int32)[:, None] * BLOCK + cols).reshape(-1)

    own_sum = jnp.stack(
        [
            jnp.take(kb, positions, axis=0).reshape(-1, heads, HEAD_DIM),
            jnp.take(vb, positions, axis=0).reshape(-1, heads, HEAD_DIM),
        ],
        axis=2,
    ).reshape(-1, 2 * half)
    all_sum = gather_blocks(own_sum, core)
    sum_count = all_sum.shape[0]
    key_block = jnp.arange(sum_count, dtype=jnp.int32) // SUMMARY
    query_block = first_block + jnp.arange(nb, dtype=jnp.int32)
    mask = (key_block[None, :] < query_block[:, None]).astype(jnp.int32)
    mask = jnp.repeat(mask, 8, axis=0)

    attended, dq, dkw, dvw, parts = attention(qb, kb, vb, gb, all_sum, mask)
    att_tok, dq_tok = to_token_layout([attended, dq], core)

    own_grad = reduce_blocks(parts, core).reshape(-1, heads, 2, HEAD_DIM)
    dk = dkw.at[positions].add(own_grad[:, :, 0].reshape(-1, half))
    dv = dvw.at[positions].add(own_grad[:, :, 1].reshape(-1, half))
    dk_tok, dv_tok = to_token_layout([dk.astype(jnp.bfloat16), dv.astype(jnp.bfloat16)], core)
    return att_tok, dq_tok, dk_tok, dv_tok


def solution(mesh):
    seq_size, head_size = mesh.devices.shape
    split = Mesh(mesh.devices.reshape(seq_size, head_size // 2, 2), ("seq", "hx", "hc"))
    tok = P(("seq", "hx", "hc"), None)
    return jax.shard_map(
        body,
        mesh=split,
        in_specs=(tok, tok, tok, tok, P("seq", None)),
        out_specs=(tok, tok, tok, tok),
        check_vma=False,
    )
```

```python
import math

import jax
import jax.numpy as jnp
from jax import lax
from jax.experimental import pallas as pl
from jax.experimental.pallas import tpu as pltpu
from jax.sharding import Mesh
from jax.sharding import PartitionSpec as P

HEAD_DIM = 128
BLOCK = 128
SUMMARY = 8

MASKED_SCORE = -1e30
GROUP = ("seq", "hx")
HEADS_PER_STEP = 4


def group_size():
    return lax.axis_size("seq") * lax.axis_size("hx")


def group_bits():
    size = group_size()
    bits = size.bit_length() - 1
    assert 1 << bits == size
    return bits


def physical_bit(core, bit):
    if core == 1 and group_bits() >= 2 and bit < 2:
        return 1 - bit
    return bit


def exchange(x, mask):
    size = group_size()
    pairs = []
    for g in range(size):
        for c in range(2):
            phys = 0
            for bit in range(group_bits()):
                if (mask >> bit) & 1:
                    phys |= 1 << physical_bit(c, bit)
            pairs.append((g * 2 + c, (g ^ phys) * 2 + c))
    return lax.ppermute(x, ("seq", "hx", "hc"), pairs)


def rounds():
    bits = list(range(group_bits()))
    return [tuple(bits[i:i + 2]) for i in range(0, len(bits), 2)]


def round_index(me, bits):
    return sum(((me >> b) & 1) << i for i, b in enumerate(bits))


def round_mask(m, bits):
    return sum(((m >> i) & 1) << b for i, b in enumerate(bits))


def swap_low_bits(x, core):
    if group_bits() < 2:
        return x
    size = x.shape[0]
    swapped = jnp.swapaxes(x.reshape((size // 4, 2, 2) + x.shape[1:]), 1, 2).reshape(x.shape)
    return jnp.where(core == 1, swapped, x)


def virtual_index(core):
    g = lax.axis_index("seq") * lax.axis_size("hx") + lax.axis_index("hx")
    if group_bits() < 2:
        return g
    swapped = (g & ~3) | ((g & 1) << 1) | ((g >> 1) & 1)
    return jnp.where(core == 1, swapped, g)


def gather_blocks(x, core):
    me = virtual_index(core)
    held = x[None]
    for bits in reversed(rounds()):
        width = 1 << len(bits)
        t_me = round_index(me, bits)
        got = jnp.stack([held] + [exchange(held, round_mask(m, bits)) for m in range(1, width)], 1)
        held = jnp.stack(
            [lax.dynamic_index_in_dim(got, t ^ t_me, 1, keepdims=False) for t in range(width)], 1
        )
        held = held.reshape((-1,) + x.shape)
    held = swap_low_bits(held, core)
    return held.reshape((-1,) + x.shape[1:])


def reduce_blocks(x, core):
    me = virtual_index(core)
    size = group_size()
    held = swap_low_bits(x.reshape((size, -1) + x.shape[1:]), core)
    for bits in rounds():
        width = 1 << len(bits)
        t_me = round_index(me, bits)
        parts = held.reshape((held.shape[0] // width, width) + held.shape[1:])
        total = lax.dynamic_index_in_dim(parts, t_me, 1, keepdims=False)
        for m in range(1, width):
            send = lax.dynamic_index_in_dim(parts, t_me ^ m, 1, keepdims=False)
            got = exchange(send.astype(jnp.bfloat16), round_mask(m, bits))
            total = total + got.astype(jnp.float32)
        held = total
    return held.reshape(x.shape[0] // size, *x.shape[1:])


def swap_with_partner(x):
    return lax.ppermute(x, "hc", [(0, 1), (1, 0)])


def to_block_layout(arrays, core):
    rows, feats = arrays[0].shape
    half = feats // 2
    mine = [lax.dynamic_slice_in_dim(a, core * half, half, 1) for a in arrays]
    theirs = [lax.dynamic_slice_in_dim(a, (1 - core) * half, half, 1) for a in arrays]
    got = swap_with_partner(jnp.concatenate(theirs, axis=1))
    out = []
    for i, m in enumerate(mine):
        r = got[:, i * half:(i + 1) * half]
        out.append(jnp.where(core == 0, jnp.concatenate([m, r], 0), jnp.concatenate([r, m], 0)))
    return out


def to_token_layout(arrays, core):
    rows2, half = arrays[0].shape
    rows = rows2 // 2
    mine = [lax.dynamic_slice_in_dim(a, core * rows, rows, 0) for a in arrays]
    theirs = [lax.dynamic_slice_in_dim(a, (1 - core) * rows, rows, 0) for a in arrays]
    got = swap_with_partner(jnp.concatenate(theirs, axis=1))
    out = []
    for i, m in enumerate(mine):
        r = got[:, i * half:(i + 1) * half]
        out.append(jnp.where(core == 0, jnp.concatenate([m, r], 1), jnp.concatenate([r, m], 1)))
    return out


def mm(a, b, trans_a=False, trans_b=False):
    dims = (((0 if trans_a else 1,), (1 if trans_b else 0,)), ((), ()))
    return lax.dot_general(a, b, dims, preferred_element_type=jnp.float32)


def attention_kernel(
    q_all, k_all, v_all, g_all, s_all, mask_ref, att_all, dq_all, dkw_all, dvw_all, ds_all
):
    j = pl.program_id(1)
    scale = 1.0 / math.sqrt(HEAD_DIM)
    f32 = jnp.float32
    bf16 = jnp.bfloat16
    allowed = mask_ref[0:1, :] > 0
    row = lax.broadcasted_iota(jnp.int32, (BLOCK, BLOCK), 0)
    col = lax.broadcasted_iota(jnp.int32, (BLOCK, BLOCK), 1)
    causal = row >= col
    for hh in range(q_all.shape[1] // HEAD_DIM):
        cols = pl.ds(hh * HEAD_DIM, HEAD_DIM)
        q = q_all[:, cols]
        k = k_all[:, cols]
        v = v_all[:, cols]
        g = g_all[:, cols]
        sk = s_all[:, pl.ds(2 * hh * HEAD_DIM, HEAD_DIM)]
        sv = s_all[:, pl.ds((2 * hh + 1) * HEAD_DIM, HEAD_DIM)]

        sw = jnp.where(causal, mm(q, k, trans_b=True) * scale, MASKED_SCORE)
        ss = jnp.where(allowed, mm(q, sk, trans_b=True) * scale, MASKED_SCORE)
        top = jnp.maximum(jnp.max(sw, axis=1, keepdims=True), jnp.max(ss, axis=1, keepdims=True))
        total = jnp.sum(jnp.exp(sw - top), axis=1, keepdims=True) + jnp.sum(
            jnp.exp(ss - top), axis=1, keepdims=True
        )
        log_norm = top + jnp.log(total)
        pw = jnp.where(causal, jnp.exp(sw - log_norm), 0.0)
        ps = jnp.where(allowed, jnp.exp(ss - log_norm), 0.0)
        pw_low = pw.astype(bf16)
        ps_low = ps.astype(bf16)
        att = (mm(pw_low, v) + mm(ps_low, sv)).astype(bf16)
        att_all[:, cols] = att
        delta = jnp.sum(g.astype(f32) * att.astype(f32), axis=1, keepdims=True)
        dsw = (pw * (mm(g, v, trans_b=True) - delta)).astype(bf16)
        dss = (ps * (mm(g, sv, trans_b=True) - delta)).astype(bf16)
        dq_all[:, cols] = ((mm(dsw, k) + mm(dss, sk)) * scale).astype(bf16)
        dkw_all[:, cols] = mm(dsw, q, trans_a=True) * scale
        dvw_all[:, cols] = mm(pw_low, g, trans_a=True)
        dks = mm(dss, q, trans_a=True) * scale
        dvs = mm(ps_low, g, trans_a=True)
        kcols = pl.ds(2 * hh * HEAD_DIM, HEAD_DIM)
        vcols = pl.ds((2 * hh + 1) * HEAD_DIM, HEAD_DIM)

        @pl.when(j == 0)
        def _():
            ds_all[:, kcols] = dks
            ds_all[:, vcols] = dvs

        @pl.when(j > 0)
        def _():
            ds_all[:, kcols] += dks
            ds_all[:, vcols] += dvs


def attention(q, k, v, g, summary, mask):
    rows, half = q.shape
    heads = half // HEAD_DIM
    nb = rows // BLOCK
    count = summary.shape[0]
    per_step = math.gcd(heads, HEADS_PER_STEP)
    tile = pl.BlockSpec((BLOCK, per_step * HEAD_DIM), lambda h, j: (j, h))
    pair = pl.BlockSpec((count, 2 * per_step * HEAD_DIM), lambda h, j: (0, h))
    bf16 = jnp.bfloat16
    f32 = jnp.float32
    flops = 2 * rows * heads * HEAD_DIM * (BLOCK + count) * 6
    return pl.pallas_call(
        attention_kernel,
        grid=(heads // per_step, nb),
        in_specs=[tile, tile, tile, tile, pair, pl.BlockSpec((8, count), lambda h, j: (j, 0))],
        out_specs=[tile, tile, tile, tile, pair],
        out_shape=[
            jax.ShapeDtypeStruct((rows, half), bf16),
            jax.ShapeDtypeStruct((rows, half), bf16),
            jax.ShapeDtypeStruct((rows, half), f32),
            jax.ShapeDtypeStruct((rows, half), f32),
            jax.ShapeDtypeStruct((count, 2 * half), f32),
        ],
        cost_estimate=pl.CostEstimate(
            flops=flops, transcendentals=rows * heads * (BLOCK + count) * 2,
            bytes_accessed=rows * half * 2 * 8 + count * half * 2 * 6,
        ),
    )(q, k, v, g, summary, mask)


def body(queries, key_rows, value_rows, out_grad, summary_columns):
    core = lax.axis_index("hc")
    hx = lax.axis_index("hx")
    shard = lax.axis_index("seq")
    score_scale = 1.0 / math.sqrt(HEAD_DIM)
    f32 = jnp.float32

    qb, kb, vb, gb = to_block_layout([queries, key_rows, value_rows, out_grad], core)
    rows, half = qb.shape
    heads = half // HEAD_DIM
    nb = rows // BLOCK
    pair_count = summary_columns.shape[0] // nb
    first_block = (shard * pair_count + hx) * nb
    cols = lax.dynamic_slice_in_dim(summary_columns, hx * nb, nb, 0)
    positions = (jnp.arange(nb, dtype=jnp.int32)[:, None] * BLOCK + cols).reshape(-1)

    own_sum = jnp.stack(
        [
            jnp.take(kb, positions, axis=0).reshape(-1, heads, HEAD_DIM),
            jnp.take(vb, positions, axis=0).reshape(-1, heads, HEAD_DIM),
        ],
        axis=2,
    ).reshape(-1, 2 * half)
    all_sum = gather_blocks(own_sum, core)
    sum_count = all_sum.shape[0]
    key_block = jnp.arange(sum_count, dtype=jnp.int32) // SUMMARY
    query_block = first_block + jnp.arange(nb, dtype=jnp.int32)
    mask = (key_block[None, :] < query_block[:, None]).astype(jnp.int32)
    mask = jnp.repeat(mask, 8, axis=0)

    attended, dq, dkw, dvw, parts = attention(qb, kb, vb, gb, all_sum, mask)
    att_tok, dq_tok = to_token_layout([attended, dq], core)

    own_grad = reduce_blocks(parts, core).reshape(-1, heads, 2, HEAD_DIM)
    dk = dkw.at[positions].add(own_grad[:, :, 0].reshape(-1, half))
    dv = dvw.at[positions].add(own_grad[:, :, 1].reshape(-1, half))
    dk_tok, dv_tok = to_token_layout([dk.astype(jnp.bfloat16), dv.astype(jnp.bfloat16)], core)
    return att_tok, dq_tok, dk_tok, dv_tok


def solution(mesh):
    seq_size, head_size = mesh.devices.shape
    split = Mesh(mesh.devices.reshape(seq_size, head_size // 2, 2), ("seq", "hx", "hc"))
    tok = P(("seq", "hx", "hc"), None)
    return jax.shard_map(
        body,
        mesh=split,
        in_specs=(tok, tok, tok, tok, P("seq", None)),
        out_specs=(tok, tok, tok, tok),
        check_vma=False,
    )
```

```python
import math

import jax
import jax.numpy as jnp
from jax import lax
from jax.experimental import pallas as pl
from jax.experimental.pallas import tpu as pltpu
from jax.sharding import Mesh
from jax.sharding import PartitionSpec as P

HEAD_DIM = 128
BLOCK = 128
SUMMARY = 8

MASKED_SCORE = -1e30
GROUP = ("seq", "hx")
HEADS_PER_STEP = 4


def group_size():
    return lax.axis_size("seq") * lax.axis_size("hx")


def group_bits():
    size = group_size()
    bits = size.bit_length() - 1
    assert 1 << bits == size
    return bits


def physical_bit(core, bit):
    if core == 1 and group_bits() >= 2 and bit < 2:
        return 1 - bit
    return bit


def exchange(x, mask):
    size = group_size()
    pairs = []
    for g in range(size):
        for c in range(2):
            phys = 0
            for bit in range(group_bits()):
                if (mask >> bit) & 1:
                    phys |= 1 << physical_bit(c, bit)
            pairs.append((g * 2 + c, (g ^ phys) * 2 + c))
    return lax.ppermute(x, ("seq", "hx", "hc"), pairs)


def rounds():
    bits = list(range(group_bits()))
    return [tuple(bits[i:i + 2]) for i in range(0, len(bits), 2)]


def round_index(me, bits):
    return sum(((me >> b) & 1) << i for i, b in enumerate(bits))


def round_mask(m, bits):
    return sum(((m >> i) & 1) << b for i, b in enumerate(bits))


def swap_low_bits(x, core):
    if group_bits() < 2:
        return x
    size = x.shape[0]
    swapped = jnp.swapaxes(x.reshape((size // 4, 2, 2) + x.shape[1:]), 1, 2).reshape(x.shape)
    return jnp.where(core == 1, swapped, x)


def virtual_index(core):
    g = lax.axis_index("seq") * lax.axis_size("hx") + lax.axis_index("hx")
    if group_bits() < 2:
        return g
    swapped = (g & ~3) | ((g & 1) << 1) | ((g >> 1) & 1)
    return jnp.where(core == 1, swapped, g)


def gather_blocks(x, core):
    me = virtual_index(core)
    held = x[None]
    for bits in reversed(rounds()):
        width = 1 << len(bits)
        t_me = round_index(me, bits)
        got = jnp.stack([held] + [exchange(held, round_mask(m, bits)) for m in range(1, width)], 1)
        held = jnp.stack(
            [lax.dynamic_index_in_dim(got, t ^ t_me, 1, keepdims=False) for t in range(width)], 1
        )
        held = held.reshape((-1,) + x.shape)
    held = swap_low_bits(held, core)
    return held.reshape((-1,) + x.shape[1:])


def reduce_blocks(x, core):
    me = virtual_index(core)
    size = group_size()
    held = swap_low_bits(x.reshape((size, -1) + x.shape[1:]), core)
    for bits in rounds():
        width = 1 << len(bits)
        t_me = round_index(me, bits)
        parts = held.reshape((held.shape[0] // width, width) + held.shape[1:])
        total = lax.dynamic_index_in_dim(parts, t_me, 1, keepdims=False)
        for m in range(1, width):
            send = lax.dynamic_index_in_dim(parts, t_me ^ m, 1, keepdims=False)
            got = exchange(send.astype(jnp.bfloat16), round_mask(m, bits))
            total = total + got.astype(jnp.float32)
        held = total
    return held.reshape(x.shape[0] // size, *x.shape[1:])


def swap_with_partner(x):
    return lax.ppermute(x, "hc", [(0, 1), (1, 0)])


def to_block_layout(arrays, core):
    rows, feats = arrays[0].shape
    half = feats // 2
    mine = [lax.dynamic_slice_in_dim(a, core * half, half, 1) for a in arrays]
    theirs = [lax.dynamic_slice_in_dim(a, (1 - core) * half, half, 1) for a in arrays]
    got = swap_with_partner(jnp.concatenate(theirs, axis=1))
    out = []
    for i, m in enumerate(mine):
        r = got[:, i * half:(i + 1) * half]
        out.append(jnp.where(core == 0, jnp.concatenate([m, r], 0), jnp.concatenate([r, m], 0)))
    return out


def to_token_layout(arrays, core):
    rows2, half = arrays[0].shape
    rows = rows2 // 2
    mine = [lax.dynamic_slice_in_dim(a, core * rows, rows, 0) for a in arrays]
    theirs = [lax.dynamic_slice_in_dim(a, (1 - core) * rows, rows, 0) for a in arrays]
    got = swap_with_partner(jnp.concatenate(theirs, axis=1))
    out = []
    for i, m in enumerate(mine):
        r = got[:, i * half:(i + 1) * half]
        out.append(jnp.where(core == 0, jnp.concatenate([m, r], 1), jnp.concatenate([r, m], 1)))
    return out


def mm(a, b, trans_a=False, trans_b=False):
    dims = (((0 if trans_a else 1,), (1 if trans_b else 0,)), ((), ()))
    return lax.dot_general(a, b, dims, preferred_element_type=jnp.float32)


def attention_kernel(
    q_all, k_all, v_all, g_all, s_all, mask_ref, att_all, dq_all, dkw_all, dvw_all, ds_all
):
    j = pl.program_id(1)
    scale = 1.0 / math.sqrt(HEAD_DIM)
    f32 = jnp.float32
    bf16 = jnp.bfloat16
    allowed = mask_ref[0:1, :] > 0
    row = lax.broadcasted_iota(jnp.int32, (BLOCK, BLOCK), 0)
    col = lax.broadcasted_iota(jnp.int32, (BLOCK, BLOCK), 1)
    causal = row >= col
    for hh in range(q_all.shape[1] // HEAD_DIM):
        cols = pl.ds(hh * HEAD_DIM, HEAD_DIM)
        q = q_all[:, cols]
        k = k_all[:, cols]
        v = v_all[:, cols]
        g = g_all[:, cols]
        sk = s_all[:, pl.ds(2 * hh * HEAD_DIM, HEAD_DIM)]
        sv = s_all[:, pl.ds((2 * hh + 1) * HEAD_DIM, HEAD_DIM)]

        sw = jnp.where(causal, mm(q, k, trans_b=True) * scale, MASKED_SCORE)
        ss = jnp.where(allowed, mm(q, sk, trans_b=True) * scale, MASKED_SCORE)
        fold = sw
        for c in range(ss.shape[1] // BLOCK):
            fold = jnp.maximum(fold, ss[:, c * BLOCK:(c + 1) * BLOCK])
        top = jnp.max(fold, axis=1, keepdims=True)
        ew = jnp.exp(sw - top)
        es = jnp.exp(ss - top)
        fold = ew
        for c in range(es.shape[1] // BLOCK):
            fold = fold + es[:, c * BLOCK:(c + 1) * BLOCK]
        inv = 1.0 / jnp.sum(fold, axis=1, keepdims=True)
        pw = ew * inv
        ps = es * inv
        pw_low = pw.astype(bf16)
        ps_low = ps.astype(bf16)
        att = (mm(pw_low, v) + mm(ps_low, sv)).astype(bf16)
        att_all[:, cols] = att
        delta = jnp.sum(g.astype(f32) * att.astype(f32), axis=1, keepdims=True)
        dsw = (pw * (mm(g, v, trans_b=True) - delta)).astype(bf16)
        dss = (ps * (mm(g, sv, trans_b=True) - delta)).astype(bf16)
        dq_all[:, cols] = ((mm(dsw, k) + mm(dss, sk)) * scale).astype(bf16)
        dkw_all[:, cols] = mm(dsw, q, trans_a=True) * scale
        dvw_all[:, cols] = mm(pw_low, g, trans_a=True)
        dks = mm(dss, q, trans_a=True) * scale
        dvs = mm(ps_low, g, trans_a=True)
        kcols = pl.ds(2 * hh * HEAD_DIM, HEAD_DIM)
        vcols = pl.ds((2 * hh + 1) * HEAD_DIM, HEAD_DIM)

        @pl.when(j == 0)
        def _():
            ds_all[:, kcols] = dks
            ds_all[:, vcols] = dvs

        @pl.when(j > 0)
        def _():
            ds_all[:, kcols] += dks
            ds_all[:, vcols] += dvs


def attention(q, k, v, g, summary, mask):
    rows, half = q.shape
    heads = half // HEAD_DIM
    nb = rows // BLOCK
    count = summary.shape[0]
    per_step = math.gcd(heads, HEADS_PER_STEP)
    tile = pl.BlockSpec((BLOCK, per_step * HEAD_DIM), lambda h, j: (j, h))
    pair = pl.BlockSpec((count, 2 * per_step * HEAD_DIM), lambda h, j: (0, h))
    bf16 = jnp.bfloat16
    f32 = jnp.float32
    flops = 2 * rows * heads * HEAD_DIM * (BLOCK + count) * 6
    return pl.pallas_call(
        attention_kernel,
        grid=(heads // per_step, nb),
        in_specs=[tile, tile, tile, tile, pair, pl.BlockSpec((8, count), lambda h, j: (j, 0))],
        out_specs=[tile, tile, tile, tile, pair],
        out_shape=[
            jax.ShapeDtypeStruct((rows, half), bf16),
            jax.ShapeDtypeStruct((rows, half), bf16),
            jax.ShapeDtypeStruct((rows, half), f32),
            jax.ShapeDtypeStruct((rows, half), f32),
            jax.ShapeDtypeStruct((count, 2 * half), f32),
        ],
        cost_estimate=pl.CostEstimate(
            flops=flops, transcendentals=rows * heads * (BLOCK + count) * 2,
            bytes_accessed=rows * half * 2 * 8 + count * half * 2 * 6,
        ),
    )(q, k, v, g, summary, mask)


def body(queries, key_rows, value_rows, out_grad, summary_columns):
    core = lax.axis_index("hc")
    hx = lax.axis_index("hx")
    shard = lax.axis_index("seq")
    score_scale = 1.0 / math.sqrt(HEAD_DIM)
    f32 = jnp.float32

    qb, kb, vb, gb = to_block_layout([queries, key_rows, value_rows, out_grad], core)
    rows, half = qb.shape
    heads = half // HEAD_DIM
    nb = rows // BLOCK
    pair_count = summary_columns.shape[0] // nb
    first_block = (shard * pair_count + hx) * nb
    cols = lax.dynamic_slice_in_dim(summary_columns, hx * nb, nb, 0)
    positions = (jnp.arange(nb, dtype=jnp.int32)[:, None] * BLOCK + cols).reshape(-1)

    own_sum = jnp.stack(
        [
            jnp.take(kb, positions, axis=0).reshape(-1, heads, HEAD_DIM),
            jnp.take(vb, positions, axis=0).reshape(-1, heads, HEAD_DIM),
        ],
        axis=2,
    ).reshape(-1, 2 * half)
    all_sum = gather_blocks(own_sum, core)
    sum_count = all_sum.shape[0]
    key_block = jnp.arange(sum_count, dtype=jnp.int32) // SUMMARY
    query_block = first_block + jnp.arange(nb, dtype=jnp.int32)
    mask = (key_block[None, :] < query_block[:, None]).astype(jnp.int32)
    mask = jnp.repeat(mask, 8, axis=0)

    attended, dq, dkw, dvw, parts = attention(qb, kb, vb, gb, all_sum, mask)
    att_tok, dq_tok = to_token_layout([attended, dq], core)

    own_grad = reduce_blocks(parts, core).reshape(-1, heads, 2, HEAD_DIM)
    dk = dkw.at[positions].add(own_grad[:, :, 0].reshape(-1, half))
    dv = dvw.at[positions].add(own_grad[:, :, 1].reshape(-1, half))
    dk_tok, dv_tok = to_token_layout([dk.astype(jnp.bfloat16), dv.astype(jnp.bfloat16)], core)
    return att_tok, dq_tok, dk_tok, dv_tok


def solution(mesh):
    seq_size, head_size = mesh.devices.shape
    split = Mesh(mesh.devices.reshape(seq_size, head_size // 2, 2), ("seq", "hx", "hc"))
    tok = P(("seq", "hx", "hc"), None)
    return jax.shard_map(
        body,
        mesh=split,
        in_specs=(tok, tok, tok, tok, P("seq", None)),
        out_specs=(tok, tok, tok, tok),
        check_vma=False,
    )
```

```python
import math

import jax
import jax.numpy as jnp
from jax import lax
from jax.experimental import pallas as pl
from jax.experimental.pallas import tpu as pltpu
from jax.sharding import Mesh
from jax.sharding import PartitionSpec as P

HEAD_DIM = 128
BLOCK = 128
SUMMARY = 8

MASKED_SCORE = -1e30
GROUP = ("seq", "hx")
HEADS_PER_STEP = 4


def group_size():
    return lax.axis_size("seq") * lax.axis_size("hx")


def group_bits():
    size = group_size()
    bits = size.bit_length() - 1
    assert 1 << bits == size
    return bits


def physical_bit(core, bit):
    if core == 1 and group_bits() >= 2 and bit < 2:
        return 1 - bit
    return bit


def exchange(x, mask):
    size = group_size()
    pairs = []
    for g in range(size):
        for c in range(2):
            phys = 0
            for bit in range(group_bits()):
                if (mask >> bit) & 1:
                    phys |= 1 << physical_bit(c, bit)
            pairs.append((g * 2 + c, (g ^ phys) * 2 + c))
    return lax.ppermute(x, ("seq", "hx", "hc"), pairs)


def rounds():
    bits = list(range(group_bits()))
    return [tuple(bits[i:i + 2]) for i in range(0, len(bits), 2)]


def round_index(me, bits):
    return sum(((me >> b) & 1) << i for i, b in enumerate(bits))


def round_mask(m, bits):
    return sum(((m >> i) & 1) << b for i, b in enumerate(bits))


def swap_low_bits(index):
    return (index & ~3) | ((index & 1) << 1) | ((index >> 1) & 1)


def virtual_index(core):
    g = lax.axis_index("seq") * lax.axis_size("hx") + lax.axis_index("hx")
    if group_bits() < 2:
        return g
    return jnp.where(core == 1, swap_low_bits(g), g)


def gather_blocks(x, core):
    me = virtual_index(core)
    held = x[None]
    for bits in reversed(rounds()):
        width = 1 << len(bits)
        t_me = round_index(me, bits)
        got = jnp.stack([held] + [exchange(held, round_mask(m, bits)) for m in range(1, width)], 1)
        held = jnp.stack(
            [lax.dynamic_index_in_dim(got, t ^ t_me, 1, keepdims=False) for t in range(width)], 1
        )
        held = held.reshape((-1,) + x.shape)
    return held.reshape((-1,) + x.shape[1:])


def reduce_blocks(x, core):
    me = virtual_index(core)
    size = group_size()
    held = x.reshape((size, -1) + x.shape[1:])
    for bits in rounds():
        width = 1 << len(bits)
        t_me = round_index(me, bits)
        parts = held.reshape((held.shape[0] // width, width) + held.shape[1:])
        total = lax.dynamic_index_in_dim(parts, t_me, 1, keepdims=False)
        for m in range(1, width):
            send = lax.dynamic_index_in_dim(parts, t_me ^ m, 1, keepdims=False)
            got = exchange(send.astype(jnp.bfloat16), round_mask(m, bits))
            total = total + got.astype(jnp.float32)
        held = total
    return held.reshape(x.shape[0] // size, *x.shape[1:])


def swap_with_partner(x):
    return lax.ppermute(x, "hc", [(0, 1), (1, 0)])


def to_block_layout(arrays, core):
    rows, feats = arrays[0].shape
    half = feats // 2
    mine = [lax.dynamic_slice_in_dim(a, core * half, half, 1) for a in arrays]
    theirs = [lax.dynamic_slice_in_dim(a, (1 - core) * half, half, 1) for a in arrays]
    got = swap_with_partner(jnp.concatenate(theirs, axis=1))
    out = []
    for i, m in enumerate(mine):
        r = got[:, i * half:(i + 1) * half]
        out.append(jnp.where(core == 0, jnp.concatenate([m, r], 0), jnp.concatenate([r, m], 0)))
    return out


def to_token_layout(arrays, core):
    rows2, half = arrays[0].shape
    rows = rows2 // 2
    mine = [lax.dynamic_slice_in_dim(a, core * rows, rows, 0) for a in arrays]
    theirs = [lax.dynamic_slice_in_dim(a, (1 - core) * rows, rows, 0) for a in arrays]
    got = swap_with_partner(jnp.concatenate(theirs, axis=1))
    out = []
    for i, m in enumerate(mine):
        r = got[:, i * half:(i + 1) * half]
        out.append(jnp.where(core == 0, jnp.concatenate([m, r], 1), jnp.concatenate([r, m], 1)))
    return out


def mm(a, b, trans_a=False, trans_b=False):
    dims = (((0 if trans_a else 1,), (1 if trans_b else 0,)), ((), ()))
    return lax.dot_general(a, b, dims, preferred_element_type=jnp.float32)


def attention_kernel(
    q_all, k_all, v_all, g_all, s_all, mask_ref, att_all, dq_all, dkw_all, dvw_all, ds_all
):
    j = pl.program_id(1)
    scale = 1.0 / math.sqrt(HEAD_DIM)
    f32 = jnp.float32
    bf16 = jnp.bfloat16
    allowed = mask_ref[0:1, :] > 0
    row = lax.broadcasted_iota(jnp.int32, (BLOCK, BLOCK), 0)
    col = lax.broadcasted_iota(jnp.int32, (BLOCK, BLOCK), 1)
    causal = row >= col
    for hh in range(q_all.shape[1] // HEAD_DIM):
        cols = pl.ds(hh * HEAD_DIM, HEAD_DIM)
        q = q_all[:, cols]
        k = k_all[:, cols]
        v = v_all[:, cols]
        g = g_all[:, cols]
        sk = s_all[:, pl.ds(2 * hh * HEAD_DIM, HEAD_DIM)]
        sv = s_all[:, pl.ds((2 * hh + 1) * HEAD_DIM, HEAD_DIM)]

        sw = jnp.where(causal, mm(q, k, trans_b=True) * scale, MASKED_SCORE)
        ss = jnp.where(allowed, mm(q, sk, trans_b=True) * scale, MASKED_SCORE)
        fold = sw
        for c in range(ss.shape[1] // BLOCK):
            fold = jnp.maximum(fold, ss[:, c * BLOCK:(c + 1) * BLOCK])
        top = jnp.max(fold, axis=1, keepdims=True)
        ew = jnp.exp(sw - top)
        es = jnp.exp(ss - top)
        fold = ew
        for c in range(es.shape[1] // BLOCK):
            fold = fold + es[:, c * BLOCK:(c + 1) * BLOCK]
        inv = 1.0 / jnp.sum(fold, axis=1, keepdims=True)
        pw = ew * inv
        ps = es * inv
        pw_low = pw.astype(bf16)
        ps_low = ps.astype(bf16)
        att = (mm(pw_low, v) + mm(ps_low, sv)).astype(bf16)
        att_all[:, cols] = att
        delta = jnp.sum(g.astype(f32) * att.astype(f32), axis=1, keepdims=True)
        dsw = (pw * (mm(g, v, trans_b=True) - delta)).astype(bf16)
        dss = (ps * (mm(g, sv, trans_b=True) - delta)).astype(bf16)
        dq_all[:, cols] = ((mm(dsw, k) + mm(dss, sk)) * scale).astype(bf16)
        dkw_all[:, cols] = mm(dsw, q, trans_a=True) * scale
        dvw_all[:, cols] = mm(pw_low, g, trans_a=True)
        dks = mm(dss, q, trans_a=True) * scale
        dvs = mm(ps_low, g, trans_a=True)
        kcols = pl.ds(2 * hh * HEAD_DIM, HEAD_DIM)
        vcols = pl.ds((2 * hh + 1) * HEAD_DIM, HEAD_DIM)

        @pl.when(j == 0)
        def _():
            ds_all[:, kcols] = dks
            ds_all[:, vcols] = dvs

        @pl.when(j > 0)
        def _():
            ds_all[:, kcols] += dks
            ds_all[:, vcols] += dvs


def attention(q, k, v, g, summary, mask):
    rows, half = q.shape
    heads = half // HEAD_DIM
    nb = rows // BLOCK
    count = summary.shape[0]
    per_step = math.gcd(heads, HEADS_PER_STEP)
    tile = pl.BlockSpec((BLOCK, per_step * HEAD_DIM), lambda h, j: (j, h))
    pair = pl.BlockSpec((count, 2 * per_step * HEAD_DIM), lambda h, j: (0, h))
    bf16 = jnp.bfloat16
    f32 = jnp.float32
    flops = 2 * rows * heads * HEAD_DIM * (BLOCK + count) * 6
    return pl.pallas_call(
        attention_kernel,
        grid=(heads // per_step, nb),
        in_specs=[tile, tile, tile, tile, pair, pl.BlockSpec((8, count), lambda h, j: (j, 0))],
        out_specs=[tile, tile, tile, tile, pair],
        out_shape=[
            jax.ShapeDtypeStruct((rows, half), bf16),
            jax.ShapeDtypeStruct((rows, half), bf16),
            jax.ShapeDtypeStruct((rows, half), f32),
            jax.ShapeDtypeStruct((rows, half), f32),
            jax.ShapeDtypeStruct((count, 2 * half), f32),
        ],
        cost_estimate=pl.CostEstimate(
            flops=flops, transcendentals=rows * heads * (BLOCK + count) * 2,
            bytes_accessed=rows * half * 2 * 8 + count * half * 2 * 6,
        ),
    )(q, k, v, g, summary, mask)


def body(queries, key_rows, value_rows, out_grad, summary_columns):
    core = lax.axis_index("hc")
    hx = lax.axis_index("hx")
    shard = lax.axis_index("seq")
    score_scale = 1.0 / math.sqrt(HEAD_DIM)
    f32 = jnp.float32

    qb, kb, vb, gb = to_block_layout([queries, key_rows, value_rows, out_grad], core)
    rows, half = qb.shape
    heads = half // HEAD_DIM
    nb = rows // BLOCK
    pair_count = summary_columns.shape[0] // nb
    first_block = (shard * pair_count + hx) * nb
    cols = lax.dynamic_slice_in_dim(summary_columns, hx * nb, nb, 0)
    positions = (jnp.arange(nb, dtype=jnp.int32)[:, None] * BLOCK + cols).reshape(-1)

    own_sum = jnp.stack(
        [
            jnp.take(kb, positions, axis=0).reshape(-1, heads, HEAD_DIM),
            jnp.take(vb, positions, axis=0).reshape(-1, heads, HEAD_DIM),
        ],
        axis=2,
    ).reshape(-1, 2 * half)
    all_sum = gather_blocks(own_sum, core)
    sum_count = all_sum.shape[0]
    slot = jnp.arange(sum_count, dtype=jnp.int32) // SUMMARY
    member = slot // nb
    if group_bits() >= 2:
        member = jnp.where(core == 1, swap_low_bits(member), member)
    key_block = member * nb + slot % nb
    query_block = first_block + jnp.arange(nb, dtype=jnp.int32)
    mask = (key_block[None, :] < query_block[:, None]).astype(jnp.int32)
    mask = jnp.repeat(mask, 8, axis=0)

    attended, dq, dkw, dvw, parts = attention(qb, kb, vb, gb, all_sum, mask)
    att_tok, dq_tok = to_token_layout([attended, dq], core)

    own_grad = reduce_blocks(parts, core).reshape(-1, heads, 2, HEAD_DIM)
    dk = dkw.at[positions].add(own_grad[:, :, 0].reshape(-1, half))
    dv = dvw.at[positions].add(own_grad[:, :, 1].reshape(-1, half))
    dk_tok, dv_tok = to_token_layout([dk.astype(jnp.bfloat16), dv.astype(jnp.bfloat16)], core)
    return att_tok, dq_tok, dk_tok, dv_tok


def solution(mesh):
    seq_size, head_size = mesh.devices.shape
    split = Mesh(mesh.devices.reshape(seq_size, head_size // 2, 2), ("seq", "hx", "hc"))
    tok = P(("seq", "hx", "hc"), None)
    return jax.shard_map(
        body,
        mesh=split,
        in_specs=(tok, tok, tok, tok, P("seq", None)),
        out_specs=(tok, tok, tok, tok),
        check_vma=False,
    )
```

```python
import math

import jax
import jax.numpy as jnp
from jax import lax
from jax.experimental import pallas as pl
from jax.experimental.pallas import tpu as pltpu
from jax.sharding import Mesh
from jax.sharding import PartitionSpec as P

HEAD_DIM = 128
BLOCK = 128
SUMMARY = 8

MASKED_SCORE = -1e30
GROUP = ("seq", "hx")
HEADS_PER_STEP = 4


def group_size():
    return lax.axis_size("seq") * lax.axis_size("hx")


def group_bits():
    size = group_size()
    bits = size.bit_length() - 1
    assert 1 << bits == size
    return bits


def physical_bit(core, bit):
    if core == 1 and group_bits() >= 2 and bit < 2:
        return 1 - bit
    return bit


def exchange(x, mask):
    size = group_size()
    pairs = []
    for g in range(size):
        for c in range(2):
            phys = 0
            for bit in range(group_bits()):
                if (mask >> bit) & 1:
                    phys |= 1 << physical_bit(c, bit)
            pairs.append((g * 2 + c, (g ^ phys) * 2 + c))
    return lax.ppermute(x, ("seq", "hx", "hc"), pairs)


def rounds():
    bits = list(range(group_bits()))
    return [tuple(bits[i:i + 2]) for i in range(0, len(bits), 2)]


def round_index(me, bits):
    return sum(((me >> b) & 1) << i for i, b in enumerate(bits))


def round_mask(m, bits):
    return sum(((m >> i) & 1) << b for i, b in enumerate(bits))


def swap_low_bits(index):
    return (index & ~3) | ((index & 1) << 1) | ((index >> 1) & 1)


def virtual_index(core):
    g = lax.axis_index("seq") * lax.axis_size("hx") + lax.axis_index("hx")
    if group_bits() < 2:
        return g
    return jnp.where(core == 1, swap_low_bits(g), g)


def gather_blocks(x, core):
    held = x[None]
    for bits in reversed(rounds()):
        width = 1 << len(bits)
        got = [held] + [exchange(held, round_mask(m, bits)) for m in range(1, width)]
        held = jnp.stack(got, 1).reshape((-1,) + x.shape)
    return held.reshape((-1,) + x.shape[1:])


def reduce_blocks(x, core):
    size = group_size()
    held = x.reshape((size, -1) + x.shape[1:])
    for bits in rounds():
        width = 1 << len(bits)
        parts = held.reshape((held.shape[0] // width, width) + held.shape[1:])
        total = parts[:, 0]
        for m in range(1, width):
            got = exchange(parts[:, m].astype(jnp.bfloat16), round_mask(m, bits))
            total = total + got.astype(jnp.float32)
        held = total
    return held.reshape(x.shape[0] // size, *x.shape[1:])


def swap_with_partner(x):
    return lax.ppermute(x, "hc", [(0, 1), (1, 0)])


def to_block_layout(arrays, core):
    rows, feats = arrays[0].shape
    half = feats // 2
    mine = [lax.dynamic_slice_in_dim(a, core * half, half, 1) for a in arrays]
    theirs = [lax.dynamic_slice_in_dim(a, (1 - core) * half, half, 1) for a in arrays]
    got = swap_with_partner(jnp.concatenate(theirs, axis=1))
    out = []
    for i, m in enumerate(mine):
        r = got[:, i * half:(i + 1) * half]
        out.append(jnp.where(core == 0, jnp.concatenate([m, r], 0), jnp.concatenate([r, m], 0)))
    return out


def to_token_layout(arrays, core):
    rows2, half = arrays[0].shape
    rows = rows2 // 2
    mine = [lax.dynamic_slice_in_dim(a, core * rows, rows, 0) for a in arrays]
    theirs = [lax.dynamic_slice_in_dim(a, (1 - core) * rows, rows, 0) for a in arrays]
    got = swap_with_partner(jnp.concatenate(theirs, axis=1))
    out = []
    for i, m in enumerate(mine):
        r = got[:, i * half:(i + 1) * half]
        out.append(jnp.where(core == 0, jnp.concatenate([m, r], 1), jnp.concatenate([r, m], 1)))
    return out


def mm(a, b, trans_a=False, trans_b=False):
    dims = (((0 if trans_a else 1,), (1 if trans_b else 0,)), ((), ()))
    return lax.dot_general(a, b, dims, preferred_element_type=jnp.float32)


def attention_kernel(
    q_all, k_all, v_all, g_all, s_all, mask_ref, att_all, dq_all, dkw_all, dvw_all, ds_all
):
    j = pl.program_id(1)
    scale = 1.0 / math.sqrt(HEAD_DIM)
    f32 = jnp.float32
    bf16 = jnp.bfloat16
    allowed = mask_ref[0:1, :] > 0
    row = lax.broadcasted_iota(jnp.int32, (BLOCK, BLOCK), 0)
    col = lax.broadcasted_iota(jnp.int32, (BLOCK, BLOCK), 1)
    causal = row >= col
    for hh in range(q_all.shape[1] // HEAD_DIM):
        cols = pl.ds(hh * HEAD_DIM, HEAD_DIM)
        q = q_all[:, cols]
        k = k_all[:, cols]
        v = v_all[:, cols]
        g = g_all[:, cols]
        sk = s_all[:, pl.ds(2 * hh * HEAD_DIM, HEAD_DIM)]
        sv = s_all[:, pl.ds((2 * hh + 1) * HEAD_DIM, HEAD_DIM)]

        sw = jnp.where(causal, mm(q, k, trans_b=True) * scale, MASKED_SCORE)
        ss = jnp.where(allowed, mm(q, sk, trans_b=True) * scale, MASKED_SCORE)
        fold = sw
        for c in range(ss.shape[1] // BLOCK):
            fold = jnp.maximum(fold, ss[:, c * BLOCK:(c + 1) * BLOCK])
        top = jnp.max(fold, axis=1, keepdims=True)
        ew = jnp.exp(sw - top)
        es = jnp.exp(ss - top)
        fold = ew
        for c in range(es.shape[1] // BLOCK):
            fold = fold + es[:, c * BLOCK:(c + 1) * BLOCK]
        inv = 1.0 / jnp.sum(fold, axis=1, keepdims=True)
        pw = ew * inv
        ps = es * inv
        pw_low = pw.astype(bf16)
        ps_low = ps.astype(bf16)
        att = (mm(pw_low, v) + mm(ps_low, sv)).astype(bf16)
        att_all[:, cols] = att
        delta = jnp.sum(g.astype(f32) * att.astype(f32), axis=1, keepdims=True)
        dsw = (pw * (mm(g, v, trans_b=True) - delta)).astype(bf16)
        dss = (ps * (mm(g, sv, trans_b=True) - delta)).astype(bf16)
        dq_all[:, cols] = ((mm(dsw, k) + mm(dss, sk)) * scale).astype(bf16)
        dkw_all[:, cols] = mm(dsw, q, trans_a=True) * scale
        dvw_all[:, cols] = mm(pw_low, g, trans_a=True)
        dks = mm(dss, q, trans_a=True) * scale
        dvs = mm(ps_low, g, trans_a=True)
        kcols = pl.ds(2 * hh * HEAD_DIM, HEAD_DIM)
        vcols = pl.ds((2 * hh + 1) * HEAD_DIM, HEAD_DIM)

        @pl.when(j == 0)
        def _():
            ds_all[:, kcols] = dks
            ds_all[:, vcols] = dvs

        @pl.when(j > 0)
        def _():
            ds_all[:, kcols] += dks
            ds_all[:, vcols] += dvs


def attention(q, k, v, g, summary, mask):
    rows, half = q.shape
    heads = half // HEAD_DIM
    nb = rows // BLOCK
    count = summary.shape[0]
    per_step = math.gcd(heads, HEADS_PER_STEP)
    tile = pl.BlockSpec((BLOCK, per_step * HEAD_DIM), lambda h, j: (j, h))
    pair = pl.BlockSpec((count, 2 * per_step * HEAD_DIM), lambda h, j: (0, h))
    bf16 = jnp.bfloat16
    f32 = jnp.float32
    flops = 2 * rows * heads * HEAD_DIM * (BLOCK + count) * 6
    return pl.pallas_call(
        attention_kernel,
        grid=(heads // per_step, nb),
        in_specs=[tile, tile, tile, tile, pair, pl.BlockSpec((8, count), lambda h, j: (j, 0))],
        out_specs=[tile, tile, tile, tile, pair],
        out_shape=[
            jax.ShapeDtypeStruct((rows, half), bf16),
            jax.ShapeDtypeStruct((rows, half), bf16),
            jax.ShapeDtypeStruct((rows, half), f32),
            jax.ShapeDtypeStruct((rows, half), f32),
            jax.ShapeDtypeStruct((count, 2 * half), f32),
        ],
        cost_estimate=pl.CostEstimate(
            flops=flops, transcendentals=rows * heads * (BLOCK + count) * 2,
            bytes_accessed=rows * half * 2 * 8 + count * half * 2 * 6,
        ),
    )(q, k, v, g, summary, mask)


def body(queries, key_rows, value_rows, out_grad, summary_columns):
    core = lax.axis_index("hc")
    hx = lax.axis_index("hx")
    shard = lax.axis_index("seq")
    score_scale = 1.0 / math.sqrt(HEAD_DIM)
    f32 = jnp.float32

    qb, kb, vb, gb = to_block_layout([queries, key_rows, value_rows, out_grad], core)
    rows, half = qb.shape
    heads = half // HEAD_DIM
    nb = rows // BLOCK
    pair_count = summary_columns.shape[0] // nb
    first_block = (shard * pair_count + hx) * nb
    cols = lax.dynamic_slice_in_dim(summary_columns, hx * nb, nb, 0)
    positions = (jnp.arange(nb, dtype=jnp.int32)[:, None] * BLOCK + cols).reshape(-1)

    own_sum = jnp.stack(
        [
            jnp.take(kb, positions, axis=0).reshape(-1, heads, HEAD_DIM),
            jnp.take(vb, positions, axis=0).reshape(-1, heads, HEAD_DIM),
        ],
        axis=2,
    ).reshape(-1, 2 * half)
    all_sum = gather_blocks(own_sum, core)
    sum_count = all_sum.shape[0]
    slot = jnp.arange(sum_count, dtype=jnp.int32) // SUMMARY
    member = (slot // nb) ^ virtual_index(core)
    if group_bits() >= 2:
        member = jnp.where(core == 1, swap_low_bits(member), member)
    key_block = member * nb + slot % nb
    query_block = first_block + jnp.arange(nb, dtype=jnp.int32)
    mask = (key_block[None, :] < query_block[:, None]).astype(jnp.int32)
    mask = jnp.repeat(mask, 8, axis=0)

    attended, dq, dkw, dvw, parts = attention(qb, kb, vb, gb, all_sum, mask)
    att_tok, dq_tok = to_token_layout([attended, dq], core)

    own_grad = reduce_blocks(parts, core).reshape(-1, heads, 2, HEAD_DIM)
    dk = dkw.at[positions].add(own_grad[:, :, 0].reshape(-1, half))
    dv = dvw.at[positions].add(own_grad[:, :, 1].reshape(-1, half))
    dk_tok, dv_tok = to_token_layout([dk.astype(jnp.bfloat16), dv.astype(jnp.bfloat16)], core)
    return att_tok, dq_tok, dk_tok, dv_tok


def solution(mesh):
    seq_size, head_size = mesh.devices.shape
    split = Mesh(mesh.devices.reshape(seq_size, head_size // 2, 2), ("seq", "hx", "hc"))
    tok = P(("seq", "hx", "hc"), None)
    return jax.shard_map(
        body,
        mesh=split,
        in_specs=(tok, tok, tok, tok, P("seq", None)),
        out_specs=(tok, tok, tok, tok),
        check_vma=False,
    )
```

```python
import math

import jax
import jax.numpy as jnp
from jax import lax
from jax.experimental import pallas as pl
from jax.experimental.pallas import tpu as pltpu
from jax.sharding import Mesh
from jax.sharding import PartitionSpec as P

HEAD_DIM = 128
BLOCK = 128
SUMMARY = 8

MASKED_SCORE = -1e30
GROUP = ("seq", "hx")
HEADS_PER_STEP = 4


def group_size():
    return lax.axis_size("seq") * lax.axis_size("hx")


def group_bits():
    size = group_size()
    bits = size.bit_length() - 1
    assert 1 << bits == size
    return bits


def physical_bit(core, bit):
    if core == 1 and group_bits() >= 2 and bit < 2:
        return 1 - bit
    return bit


def exchange(x, mask):
    size = group_size()
    pairs = []
    for g in range(size):
        for c in range(2):
            phys = 0
            for bit in range(group_bits()):
                if (mask >> bit) & 1:
                    phys |= 1 << physical_bit(c, bit)
            pairs.append((g * 2 + c, (g ^ phys) * 2 + c))
    return lax.ppermute(x, ("seq", "hx", "hc"), pairs)


def rounds():
    bits = list(range(group_bits()))
    return [tuple(bits[i:i + 2]) for i in range(0, len(bits), 2)]


def round_index(me, bits):
    return sum(((me >> b) & 1) << i for i, b in enumerate(bits))


def round_mask(m, bits):
    return sum(((m >> i) & 1) << b for i, b in enumerate(bits))


def swap_low_bits(index):
    return (index & ~3) | ((index & 1) << 1) | ((index >> 1) & 1)


def virtual_index(core):
    g = lax.axis_index("seq") * lax.axis_size("hx") + lax.axis_index("hx")
    if group_bits() < 2:
        return g
    return jnp.where(core == 1, swap_low_bits(g), g)


def gather_blocks(x, core):
    held = x[None]
    for bits in reversed(rounds()):
        width = 1 << len(bits)
        got = [held] + [exchange(held, round_mask(m, bits)) for m in range(1, width)]
        held = jnp.stack(got, 1).reshape((-1,) + x.shape)
    return held.reshape((-1,) + x.shape[1:])


def reduce_blocks(x, core):
    size = group_size()
    held = x.reshape((size, -1) + x.shape[1:])
    for bits in rounds():
        width = 1 << len(bits)
        parts = held.reshape((held.shape[0] // width, width) + held.shape[1:])
        total = parts[:, 0].astype(jnp.float32)
        for m in range(1, width):
            got = exchange(parts[:, m].astype(jnp.bfloat16), round_mask(m, bits))
            total = total + got.astype(jnp.float32)
        held = total
    return held.reshape(x.shape[0] // size, *x.shape[1:])


def swap_with_partner(x):
    return lax.ppermute(x, "hc", [(0, 1), (1, 0)])


def to_block_layout(arrays, core):
    rows, feats = arrays[0].shape
    half = feats // 2
    mine = [lax.dynamic_slice_in_dim(a, core * half, half, 1) for a in arrays]
    theirs = [lax.dynamic_slice_in_dim(a, (1 - core) * half, half, 1) for a in arrays]
    got = swap_with_partner(jnp.concatenate(theirs, axis=1))
    out = []
    for i, m in enumerate(mine):
        r = got[:, i * half:(i + 1) * half]
        out.append(jnp.where(core == 0, jnp.concatenate([m, r], 0), jnp.concatenate([r, m], 0)))
    return out


def to_token_layout(arrays, core):
    rows2, half = arrays[0].shape
    rows = rows2 // 2
    mine = [lax.dynamic_slice_in_dim(a, core * rows, rows, 0) for a in arrays]
    theirs = [lax.dynamic_slice_in_dim(a, (1 - core) * rows, rows, 0) for a in arrays]
    got = swap_with_partner(jnp.concatenate(theirs, axis=1))
    out = []
    for i, m in enumerate(mine):
        r = got[:, i * half:(i + 1) * half]
        out.append(jnp.where(core == 0, jnp.concatenate([m, r], 1), jnp.concatenate([r, m], 1)))
    return out


def mm(a, b, trans_a=False, trans_b=False):
    dims = (((0 if trans_a else 1,), (1 if trans_b else 0,)), ((), ()))
    return lax.dot_general(a, b, dims, preferred_element_type=jnp.float32)


def attention_kernel(
    q_all, k_all, v_all, g_all, s_all, mask_ref, att_all, dq_all, dkw_all, dvw_all, ds_out, ds_all
):
    j = pl.program_id(1)
    scale = 1.0 / math.sqrt(HEAD_DIM)
    f32 = jnp.float32
    bf16 = jnp.bfloat16
    allowed = mask_ref[0:1, :] > 0
    row = lax.broadcasted_iota(jnp.int32, (BLOCK, BLOCK), 0)
    col = lax.broadcasted_iota(jnp.int32, (BLOCK, BLOCK), 1)
    causal = row >= col
    for hh in range(q_all.shape[1] // HEAD_DIM):
        cols = pl.ds(hh * HEAD_DIM, HEAD_DIM)
        q = q_all[:, cols]
        k = k_all[:, cols]
        v = v_all[:, cols]
        g = g_all[:, cols]
        sk = s_all[:, pl.ds(2 * hh * HEAD_DIM, HEAD_DIM)]
        sv = s_all[:, pl.ds((2 * hh + 1) * HEAD_DIM, HEAD_DIM)]

        sw = jnp.where(causal, mm(q, k, trans_b=True) * scale, MASKED_SCORE)
        ss = jnp.where(allowed, mm(q, sk, trans_b=True) * scale, MASKED_SCORE)
        fold = sw
        for c in range(ss.shape[1] // BLOCK):
            fold = jnp.maximum(fold, ss[:, c * BLOCK:(c + 1) * BLOCK])
        top = jnp.max(fold, axis=1, keepdims=True)
        ew = jnp.exp(sw - top)
        es = jnp.exp(ss - top)
        fold = ew
        for c in range(es.shape[1] // BLOCK):
            fold = fold + es[:, c * BLOCK:(c + 1) * BLOCK]
        inv = 1.0 / jnp.sum(fold, axis=1, keepdims=True)
        pw = ew * inv
        ps = es * inv
        pw_low = pw.astype(bf16)
        ps_low = ps.astype(bf16)
        att = (mm(pw_low, v) + mm(ps_low, sv)).astype(bf16)
        att_all[:, cols] = att
        delta = jnp.sum(g.astype(f32) * att.astype(f32), axis=1, keepdims=True)
        dsw = (pw * (mm(g, v, trans_b=True) - delta)).astype(bf16)
        dss = (ps * (mm(g, sv, trans_b=True) - delta)).astype(bf16)
        dq_all[:, cols] = ((mm(dsw, k) + mm(dss, sk)) * scale).astype(bf16)
        dkw_all[:, cols] = mm(dsw, q, trans_a=True) * scale
        dvw_all[:, cols] = mm(pw_low, g, trans_a=True)
        dks = mm(dss, q, trans_a=True) * scale
        dvs = mm(ps_low, g, trans_a=True)
        kcols = pl.ds(2 * hh * HEAD_DIM, HEAD_DIM)
        vcols = pl.ds((2 * hh + 1) * HEAD_DIM, HEAD_DIM)

        @pl.when(j == 0)
        def _():
            ds_all[:, kcols] = dks
            ds_all[:, vcols] = dvs

        @pl.when(j > 0)
        def _():
            ds_all[:, kcols] += dks
            ds_all[:, vcols] += dvs

    @pl.when(j == pl.num_programs(1) - 1)
    def _():
        ds_out[...] = ds_all[...].astype(ds_out.dtype)


def attention(q, k, v, g, summary, mask):
    rows, half = q.shape
    heads = half // HEAD_DIM
    nb = rows // BLOCK
    count = summary.shape[0]
    per_step = math.gcd(heads, HEADS_PER_STEP)
    tile = pl.BlockSpec((BLOCK, per_step * HEAD_DIM), lambda h, j: (j, h))
    pair = pl.BlockSpec((count, 2 * per_step * HEAD_DIM), lambda h, j: (0, h))
    bf16 = jnp.bfloat16
    f32 = jnp.float32
    flops = 2 * rows * heads * HEAD_DIM * (BLOCK + count) * 6
    return pl.pallas_call(
        attention_kernel,
        grid=(heads // per_step, nb),
        in_specs=[tile, tile, tile, tile, pair, pl.BlockSpec((8, count), lambda h, j: (j, 0))],
        out_specs=[tile, tile, tile, tile, pair],
        out_shape=[
            jax.ShapeDtypeStruct((rows, half), bf16),
            jax.ShapeDtypeStruct((rows, half), bf16),
            jax.ShapeDtypeStruct((rows, half), f32),
            jax.ShapeDtypeStruct((rows, half), f32),
            jax.ShapeDtypeStruct((count, 2 * half), bf16),
        ],
        scratch_shapes=[pltpu.VMEM((count, 2 * per_step * HEAD_DIM), f32)],
        cost_estimate=pl.CostEstimate(
            flops=flops, transcendentals=rows * heads * (BLOCK + count) * 2,
            bytes_accessed=rows * half * 2 * 8 + count * half * 2 * 6,
        ),
    )(q, k, v, g, summary, mask)


def body(queries, key_rows, value_rows, out_grad, summary_columns):
    core = lax.axis_index("hc")
    hx = lax.axis_index("hx")
    shard = lax.axis_index("seq")
    score_scale = 1.0 / math.sqrt(HEAD_DIM)
    f32 = jnp.float32

    qb, kb, vb, gb = to_block_layout([queries, key_rows, value_rows, out_grad], core)
    rows, half = qb.shape
    heads = half // HEAD_DIM
    nb = rows // BLOCK
    pair_count = summary_columns.shape[0] // nb
    first_block = (shard * pair_count + hx) * nb
    cols = lax.dynamic_slice_in_dim(summary_columns, hx * nb, nb, 0)
    positions = (jnp.arange(nb, dtype=jnp.int32)[:, None] * BLOCK + cols).reshape(-1)

    own_sum = jnp.stack(
        [
            jnp.take(kb, positions, axis=0).reshape(-1, heads, HEAD_DIM),
            jnp.take(vb, positions, axis=0).reshape(-1, heads, HEAD_DIM),
        ],
        axis=2,
    ).reshape(-1, 2 * half)
    all_sum = gather_blocks(own_sum, core)
    sum_count = all_sum.shape[0]
    slot = jnp.arange(sum_count, dtype=jnp.int32) // SUMMARY
    member = (slot // nb) ^ virtual_index(core)
    if group_bits() >= 2:
        member = jnp.where(core == 1, swap_low_bits(member), member)
    key_block = member * nb + slot % nb
    query_block = first_block + jnp.arange(nb, dtype=jnp.int32)
    mask = (key_block[None, :] < query_block[:, None]).astype(jnp.int32)
    mask = jnp.repeat(mask, 8, axis=0)

    attended, dq, dkw, dvw, parts = attention(qb, kb, vb, gb, all_sum, mask)
    att_tok, dq_tok = to_token_layout([attended, dq], core)

    own_grad = reduce_blocks(parts, core).reshape(-1, heads, 2, HEAD_DIM)
    dk = dkw.at[positions].add(own_grad[:, :, 0].reshape(-1, half))
    dv = dvw.at[positions].add(own_grad[:, :, 1].reshape(-1, half))
    dk_tok, dv_tok = to_token_layout([dk.astype(jnp.bfloat16), dv.astype(jnp.bfloat16)], core)
    return att_tok, dq_tok, dk_tok, dv_tok


def solution(mesh):
    seq_size, head_size = mesh.devices.shape
    split = Mesh(mesh.devices.reshape(seq_size, head_size // 2, 2), ("seq", "hx", "hc"))
    tok = P(("seq", "hx", "hc"), None)
    return jax.shard_map(
        body,
        mesh=split,
        in_specs=(tok, tok, tok, tok, P("seq", None)),
        out_specs=(tok, tok, tok, tok),
        check_vma=False,
    )
```

```python
import math

import jax
import jax.numpy as jnp
from jax import lax
from jax.experimental import pallas as pl
from jax.experimental.pallas import tpu as pltpu
from jax.sharding import Mesh
from jax.sharding import PartitionSpec as P

HEAD_DIM = 128
BLOCK = 128
SUMMARY = 8

MASKED_SCORE = -1e30
GROUP = ("seq", "hx")
HEADS_PER_STEP = 4


def group_size():
    return lax.axis_size("seq") * lax.axis_size("hx")


def group_bits():
    size = group_size()
    bits = size.bit_length() - 1
    assert 1 << bits == size
    return bits


def physical_bit(core, bit):
    if core == 1 and group_bits() >= 2 and bit < 2:
        return 1 - bit
    return bit


def exchange(x, mask):
    size = group_size()
    pairs = []
    for g in range(size):
        for c in range(2):
            phys = 0
            for bit in range(group_bits()):
                if (mask >> bit) & 1:
                    phys |= 1 << physical_bit(c, bit)
            pairs.append((g * 2 + c, (g ^ phys) * 2 + c))
    return lax.ppermute(x, ("seq", "hx", "hc"), pairs)


def rounds():
    bits = list(range(group_bits()))
    return [tuple(bits[i:i + 2]) for i in range(0, len(bits), 2)]


def round_index(me, bits):
    return sum(((me >> b) & 1) << i for i, b in enumerate(bits))


def exchange_member(index):
    out = 0
    rest = index
    for bits in reversed(rounds()):
        width = 1 << len(bits)
        out = out + (rest % width) * (1 << bits[0])
        rest = rest // width
    return out


def round_mask(m, bits):
    return sum(((m >> i) & 1) << b for i, b in enumerate(bits))


def swap_low_bits(index):
    return (index & ~3) | ((index & 1) << 1) | ((index >> 1) & 1)


def virtual_index(core):
    g = lax.axis_index("seq") * lax.axis_size("hx") + lax.axis_index("hx")
    if group_bits() < 2:
        return g
    return jnp.where(core == 1, swap_low_bits(g), g)


def gather_blocks(x, core):
    held = x[None]
    for bits in reversed(rounds()):
        width = 1 << len(bits)
        got = [held] + [exchange(held, round_mask(m, bits)) for m in range(1, width)]
        held = jnp.concatenate(got, 0)
    return held.reshape((-1,) + x.shape[1:])


def reduce_blocks(x, core):
    size = group_size()
    held = x.reshape((size, -1) + x.shape[1:])
    for bits in rounds():
        width = 1 << len(bits)
        parts = held.reshape((width, held.shape[0] // width) + held.shape[1:])
        total = parts[0].astype(jnp.float32)
        for m in range(1, width):
            got = exchange(parts[m].astype(jnp.bfloat16), round_mask(m, bits))
            total = total + got.astype(jnp.float32)
        held = total
    return held.reshape(x.shape[0] // size, *x.shape[1:])


def swap_with_partner(x):
    return lax.ppermute(x, "hc", [(0, 1), (1, 0)])


def to_block_layout(arrays, core):
    rows, feats = arrays[0].shape
    half = feats // 2
    mine = [lax.dynamic_slice_in_dim(a, core * half, half, 1) for a in arrays]
    theirs = [lax.dynamic_slice_in_dim(a, (1 - core) * half, half, 1) for a in arrays]
    got = swap_with_partner(jnp.concatenate(theirs, axis=1))
    out = []
    for i, m in enumerate(mine):
        r = got[:, i * half:(i + 1) * half]
        out.append(jnp.where(core == 0, jnp.concatenate([m, r], 0), jnp.concatenate([r, m], 0)))
    return out


def to_token_layout(arrays, core):
    rows2, half = arrays[0].shape
    rows = rows2 // 2
    mine = [lax.dynamic_slice_in_dim(a, core * rows, rows, 0) for a in arrays]
    theirs = [lax.dynamic_slice_in_dim(a, (1 - core) * rows, rows, 0) for a in arrays]
    got = swap_with_partner(jnp.concatenate(theirs, axis=1))
    out = []
    for i, m in enumerate(mine):
        r = got[:, i * half:(i + 1) * half]
        out.append(jnp.where(core == 0, jnp.concatenate([m, r], 1), jnp.concatenate([r, m], 1)))
    return out


def mm(a, b, trans_a=False, trans_b=False):
    dims = (((0 if trans_a else 1,), (1 if trans_b else 0,)), ((), ()))
    return lax.dot_general(a, b, dims, preferred_element_type=jnp.float32)


def attention_kernel(
    q_all, k_all, v_all, g_all, s_all, mask_ref, att_all, dq_all, dkw_all, dvw_all, ds_out, ds_all
):
    j = pl.program_id(1)
    scale = 1.0 / math.sqrt(HEAD_DIM)
    f32 = jnp.float32
    bf16 = jnp.bfloat16
    allowed = mask_ref[0:1, :] > 0
    row = lax.broadcasted_iota(jnp.int32, (BLOCK, BLOCK), 0)
    col = lax.broadcasted_iota(jnp.int32, (BLOCK, BLOCK), 1)
    causal = row >= col
    for hh in range(q_all.shape[1] // HEAD_DIM):
        cols = pl.ds(hh * HEAD_DIM, HEAD_DIM)
        q = q_all[:, cols]
        k = k_all[:, cols]
        v = v_all[:, cols]
        g = g_all[:, cols]
        sk = s_all[:, pl.ds(2 * hh * HEAD_DIM, HEAD_DIM)]
        sv = s_all[:, pl.ds((2 * hh + 1) * HEAD_DIM, HEAD_DIM)]

        sw = jnp.where(causal, mm(q, k, trans_b=True) * scale, MASKED_SCORE)
        ss = jnp.where(allowed, mm(q, sk, trans_b=True) * scale, MASKED_SCORE)
        fold = sw
        for c in range(ss.shape[1] // BLOCK):
            fold = jnp.maximum(fold, ss[:, c * BLOCK:(c + 1) * BLOCK])
        top = jnp.max(fold, axis=1, keepdims=True)
        ew = jnp.exp(sw - top)
        es = jnp.exp(ss - top)
        fold = ew
        for c in range(es.shape[1] // BLOCK):
            fold = fold + es[:, c * BLOCK:(c + 1) * BLOCK]
        inv = 1.0 / jnp.sum(fold, axis=1, keepdims=True)
        pw = ew * inv
        ps = es * inv
        pw_low = pw.astype(bf16)
        ps_low = ps.astype(bf16)
        att = (mm(pw_low, v) + mm(ps_low, sv)).astype(bf16)
        att_all[:, cols] = att
        delta = jnp.sum(g.astype(f32) * att.astype(f32), axis=1, keepdims=True)
        dsw = (pw * (mm(g, v, trans_b=True) - delta)).astype(bf16)
        dss = (ps * (mm(g, sv, trans_b=True) - delta)).astype(bf16)
        dq_all[:, cols] = ((mm(dsw, k) + mm(dss, sk)) * scale).astype(bf16)
        dkw_all[:, cols] = mm(dsw, q, trans_a=True) * scale
        dvw_all[:, cols] = mm(pw_low, g, trans_a=True)
        dks = mm(dss, q, trans_a=True) * scale
        dvs = mm(ps_low, g, trans_a=True)
        kcols = pl.ds(2 * hh * HEAD_DIM, HEAD_DIM)
        vcols = pl.ds((2 * hh + 1) * HEAD_DIM, HEAD_DIM)

        @pl.when(j == 0)
        def _():
            ds_all[:, kcols] = dks
            ds_all[:, vcols] = dvs

        @pl.when(j > 0)
        def _():
            ds_all[:, kcols] += dks
            ds_all[:, vcols] += dvs

    @pl.when(j == pl.num_programs(1) - 1)
    def _():
        ds_out[...] = ds_all[...].astype(ds_out.dtype)


def attention(q, k, v, g, summary, mask):
    rows, half = q.shape
    heads = half // HEAD_DIM
    nb = rows // BLOCK
    count = summary.shape[0]
    per_step = math.gcd(heads, HEADS_PER_STEP)
    tile = pl.BlockSpec((BLOCK, per_step * HEAD_DIM), lambda h, j: (j, h))
    pair = pl.BlockSpec((count, 2 * per_step * HEAD_DIM), lambda h, j: (0, h))
    bf16 = jnp.bfloat16
    f32 = jnp.float32
    flops = 2 * rows * heads * HEAD_DIM * (BLOCK + count) * 6
    return pl.pallas_call(
        attention_kernel,
        grid=(heads // per_step, nb),
        in_specs=[tile, tile, tile, tile, pair, pl.BlockSpec((8, count), lambda h, j: (j, 0))],
        out_specs=[tile, tile, tile, tile, pair],
        out_shape=[
            jax.ShapeDtypeStruct((rows, half), bf16),
            jax.ShapeDtypeStruct((rows, half), bf16),
            jax.ShapeDtypeStruct((rows, half), f32),
            jax.ShapeDtypeStruct((rows, half), f32),
            jax.ShapeDtypeStruct((count, 2 * half), bf16),
        ],
        scratch_shapes=[pltpu.VMEM((count, 2 * per_step * HEAD_DIM), f32)],
        cost_estimate=pl.CostEstimate(
            flops=flops, transcendentals=rows * heads * (BLOCK + count) * 2,
            bytes_accessed=rows * half * 2 * 8 + count * half * 2 * 6,
        ),
    )(q, k, v, g, summary, mask)


def body(queries, key_rows, value_rows, out_grad, summary_columns):
    core = lax.axis_index("hc")
    hx = lax.axis_index("hx")
    shard = lax.axis_index("seq")
    score_scale = 1.0 / math.sqrt(HEAD_DIM)
    f32 = jnp.float32

    qb, kb, vb, gb = to_block_layout([queries, key_rows, value_rows, out_grad], core)
    rows, half = qb.shape
    heads = half // HEAD_DIM
    nb = rows // BLOCK
    pair_count = summary_columns.shape[0] // nb
    first_block = (shard * pair_count + hx) * nb
    cols = lax.dynamic_slice_in_dim(summary_columns, hx * nb, nb, 0)
    positions = (jnp.arange(nb, dtype=jnp.int32)[:, None] * BLOCK + cols).reshape(-1)

    own_sum = jnp.stack(
        [
            jnp.take(kb, positions, axis=0).reshape(-1, heads, HEAD_DIM),
            jnp.take(vb, positions, axis=0).reshape(-1, heads, HEAD_DIM),
        ],
        axis=2,
    ).reshape(-1, 2 * half)
    all_sum = gather_blocks(own_sum, core)
    sum_count = all_sum.shape[0]
    slot = jnp.arange(sum_count, dtype=jnp.int32) // SUMMARY
    member = exchange_member(slot // nb) ^ virtual_index(core)
    if group_bits() >= 2:
        member = jnp.where(core == 1, swap_low_bits(member), member)
    key_block = member * nb + slot % nb
    query_block = first_block + jnp.arange(nb, dtype=jnp.int32)
    mask = (key_block[None, :] < query_block[:, None]).astype(jnp.int32)
    mask = jnp.repeat(mask, 8, axis=0)

    attended, dq, dkw, dvw, parts = attention(qb, kb, vb, gb, all_sum, mask)
    att_tok, dq_tok = to_token_layout([attended, dq], core)

    own_grad = reduce_blocks(parts, core).reshape(-1, heads, 2, HEAD_DIM)
    dk = dkw.at[positions].add(own_grad[:, :, 0].reshape(-1, half))
    dv = dvw.at[positions].add(own_grad[:, :, 1].reshape(-1, half))
    dk_tok, dv_tok = to_token_layout([dk.astype(jnp.bfloat16), dv.astype(jnp.bfloat16)], core)
    return att_tok, dq_tok, dk_tok, dv_tok


def solution(mesh):
    seq_size, head_size = mesh.devices.shape
    split = Mesh(mesh.devices.reshape(seq_size, head_size // 2, 2), ("seq", "hx", "hc"))
    tok = P(("seq", "hx", "hc"), None)
    return jax.shard_map(
        body,
        mesh=split,
        in_specs=(tok, tok, tok, tok, P("seq", None)),
        out_specs=(tok, tok, tok, tok),
        check_vma=False,
    )
```

```python
import math

import jax
import jax.numpy as jnp
from jax import lax
from jax.experimental import pallas as pl
from jax.experimental.pallas import tpu as pltpu
from jax.sharding import Mesh
from jax.sharding import PartitionSpec as P

HEAD_DIM = 128
BLOCK = 128
SUMMARY = 8

MASKED_SCORE = -1e30
GROUP = ("seq", "hx")
HEADS_PER_STEP = 4


def group_size():
    return lax.axis_size("seq") * lax.axis_size("hx")


def group_bits():
    size = group_size()
    bits = size.bit_length() - 1
    assert 1 << bits == size
    return bits


def physical_bit(core, bit):
    if core == 1 and group_bits() >= 2 and bit < 2:
        return 1 - bit
    return bit


def exchange(x, mask):
    size = group_size()
    pairs = []
    for g in range(size):
        for c in range(2):
            phys = 0
            for bit in range(group_bits()):
                if (mask >> bit) & 1:
                    phys |= 1 << physical_bit(c, bit)
            pairs.append((g * 2 + c, (g ^ phys) * 2 + c))
    return lax.ppermute(x, ("seq", "hx", "hc"), pairs)


def rounds():
    bits = list(range(group_bits()))
    return [tuple(bits[i:i + 2]) for i in range(0, len(bits), 2)]


def round_index(me, bits):
    return sum(((me >> b) & 1) << i for i, b in enumerate(bits))


def round_mask(m, bits):
    return sum(((m >> i) & 1) << b for i, b in enumerate(bits))


def swap_low_bits(index):
    return (index & ~3) | ((index & 1) << 1) | ((index >> 1) & 1)


def virtual_index(core):
    g = lax.axis_index("seq") * lax.axis_size("hx") + lax.axis_index("hx")
    if group_bits() < 2:
        return g
    return jnp.where(core == 1, swap_low_bits(g), g)


def gather_blocks(x, core):
    held = x[None]
    for bits in reversed(rounds()):
        width = 1 << len(bits)
        got = [held] + [exchange(held, round_mask(m, bits)) for m in range(1, width)]
        held = jnp.stack(got, 1).reshape((-1,) + x.shape)
    return held.reshape((-1,) + x.shape[1:])


def reduce_blocks(x, core):
    size = group_size()
    held = x.reshape((size, -1) + x.shape[1:])
    for bits in rounds():
        width = 1 << len(bits)
        parts = held.reshape((held.shape[0] // width, width) + held.shape[1:])
        total = parts[:, 0]
        for m in range(1, width):
            got = exchange(parts[:, m].astype(jnp.bfloat16), round_mask(m, bits))
            total = total + got.astype(jnp.float32)
        held = total
    return held.reshape(x.shape[0] // size, *x.shape[1:])


def swap_with_partner(x):
    return lax.ppermute(x, "hc", [(0, 1), (1, 0)])


def to_block_layout(arrays, core):
    rows, feats = arrays[0].shape
    half = feats // 2
    mine = [lax.dynamic_slice_in_dim(a, core * half, half, 1) for a in arrays]
    theirs = [lax.dynamic_slice_in_dim(a, (1 - core) * half, half, 1) for a in arrays]
    got = swap_with_partner(jnp.concatenate(theirs, axis=1))
    out = []
    for i, m in enumerate(mine):
        r = got[:, i * half:(i + 1) * half]
        out.append(jnp.where(core == 0, jnp.concatenate([m, r], 0), jnp.concatenate([r, m], 0)))
    return out


def to_token_layout(arrays, core):
    rows2, half = arrays[0].shape
    rows = rows2 // 2
    mine = [lax.dynamic_slice_in_dim(a, core * rows, rows, 0) for a in arrays]
    theirs = [lax.dynamic_slice_in_dim(a, (1 - core) * rows, rows, 0) for a in arrays]
    got = swap_with_partner(jnp.concatenate(theirs, axis=1))
    out = []
    for i, m in enumerate(mine):
        r = got[:, i * half:(i + 1) * half]
        out.append(jnp.where(core == 0, jnp.concatenate([m, r], 1), jnp.concatenate([r, m], 1)))
    return out


def mm(a, b, trans_a=False, trans_b=False):
    dims = (((0 if trans_a else 1,), (1 if trans_b else 0,)), ((), ()))
    return lax.dot_general(a, b, dims, preferred_element_type=jnp.float32)


def attention_kernel(
    q_all, k_all, v_all, g_all, s_all, mask_ref, att_all, dq_all, dkw_all, dvw_all, ds_all
):
    j = pl.program_id(1)
    scale = 1.0 / math.sqrt(HEAD_DIM)
    f32 = jnp.float32
    bf16 = jnp.bfloat16
    allowed = mask_ref[0:1, :] > 0
    row = lax.broadcasted_iota(jnp.int32, (BLOCK, BLOCK), 0)
    col = lax.broadcasted_iota(jnp.int32, (BLOCK, BLOCK), 1)
    causal = row >= col
    for hh in range(q_all.shape[1] // HEAD_DIM):
        cols = pl.ds(hh * HEAD_DIM, HEAD_DIM)
        q = q_all[:, cols]
        k = k_all[:, cols]
        v = v_all[:, cols]
        g = g_all[:, cols]
        sk = s_all[:, pl.ds(2 * hh * HEAD_DIM, HEAD_DIM)]
        sv = s_all[:, pl.ds((2 * hh + 1) * HEAD_DIM, HEAD_DIM)]

        sw = jnp.where(causal, mm(q, k, trans_b=True) * scale, MASKED_SCORE)
        ss = jnp.where(allowed, mm(q, sk, trans_b=True) * scale, MASKED_SCORE)
        fold = sw
        for c in range(ss.shape[1] // BLOCK):
            fold = jnp.maximum(fold, ss[:, c * BLOCK:(c + 1) * BLOCK])
        top = jnp.max(fold, axis=1, keepdims=True)
        ew = jnp.exp(sw - top)
        es = jnp.exp(ss - top)
        fold = ew
        for c in range(es.shape[1] // BLOCK):
            fold = fold + es[:, c * BLOCK:(c + 1) * BLOCK]
        inv = 1.0 / jnp.sum(fold, axis=1, keepdims=True)
        pw = ew * inv
        ps = es * inv
        pw_low = pw.astype(bf16)
        ps_low = ps.astype(bf16)
        att = (mm(pw_low, v) + mm(ps_low, sv)).astype(bf16)
        att_all[:, cols] = att
        delta = jnp.sum(g.astype(f32) * att.astype(f32), axis=1, keepdims=True)
        dsw = (pw * (mm(g, v, trans_b=True) - delta)).astype(bf16)
        dss = (ps * (mm(g, sv, trans_b=True) - delta)).astype(bf16)
        dq_all[:, cols] = ((mm(dsw, k) + mm(dss, sk)) * scale).astype(bf16)
        dkw_all[:, cols] = mm(dsw, q, trans_a=True) * scale
        dvw_all[:, cols] = mm(pw_low, g, trans_a=True)
        dks = mm(dss, q, trans_a=True) * scale
        dvs = mm(ps_low, g, trans_a=True)
        kcols = pl.ds(2 * hh * HEAD_DIM, HEAD_DIM)
        vcols = pl.ds((2 * hh + 1) * HEAD_DIM, HEAD_DIM)

        @pl.when(j == 0)
        def _():
            ds_all[:, kcols] = dks
            ds_all[:, vcols] = dvs

        @pl.when(j > 0)
        def _():
            ds_all[:, kcols] += dks
            ds_all[:, vcols] += dvs


def attention(q, k, v, g, summary, mask):
    rows, half = q.shape
    heads = half // HEAD_DIM
    nb = rows // BLOCK
    count = summary.shape[0]
    per_step = math.gcd(heads, HEADS_PER_STEP)
    tile = pl.BlockSpec((BLOCK, per_step * HEAD_DIM), lambda h, j: (j, h))
    pair = pl.BlockSpec((count, 2 * per_step * HEAD_DIM), lambda h, j: (0, h))
    bf16 = jnp.bfloat16
    f32 = jnp.float32
    flops = 2 * rows * heads * HEAD_DIM * (BLOCK + count) * 6
    return pl.pallas_call(
        attention_kernel,
        grid=(heads // per_step, nb),
        in_specs=[tile, tile, tile, tile, pair, pl.BlockSpec((8, count), lambda h, j: (j, 0))],
        out_specs=[tile, tile, tile, tile, pair],
        out_shape=[
            jax.ShapeDtypeStruct((rows, half), bf16),
            jax.ShapeDtypeStruct((rows, half), bf16),
            jax.ShapeDtypeStruct((rows, half), f32),
            jax.ShapeDtypeStruct((rows, half), f32),
            jax.ShapeDtypeStruct((count, 2 * half), f32),
        ],
        cost_estimate=pl.CostEstimate(
            flops=flops, transcendentals=rows * heads * (BLOCK + count) * 2,
            bytes_accessed=rows * half * 2 * 8 + count * half * 2 * 6,
        ),
    )(q, k, v, g, summary, mask)


def body(queries, key_rows, value_rows, out_grad, summary_columns):
    core = lax.axis_index("hc")
    hx = lax.axis_index("hx")
    shard = lax.axis_index("seq")
    score_scale = 1.0 / math.sqrt(HEAD_DIM)
    f32 = jnp.float32

    kb, vb = to_block_layout([key_rows, value_rows], core)
    qb, gb = to_block_layout([queries, out_grad], core)
    rows, half = qb.shape
    heads = half // HEAD_DIM
    nb = rows // BLOCK
    pair_count = summary_columns.shape[0] // nb
    first_block = (shard * pair_count + hx) * nb
    cols = lax.dynamic_slice_in_dim(summary_columns, hx * nb, nb, 0)
    positions = (jnp.arange(nb, dtype=jnp.int32)[:, None] * BLOCK + cols).reshape(-1)

    own_sum = jnp.stack(
        [
            jnp.take(kb, positions, axis=0).reshape(-1, heads, HEAD_DIM),
            jnp.take(vb, positions, axis=0).reshape(-1, heads, HEAD_DIM),
        ],
        axis=2,
    ).reshape(-1, 2 * half)
    all_sum = gather_blocks(own_sum, core)
    sum_count = all_sum.shape[0]
    slot = jnp.arange(sum_count, dtype=jnp.int32) // SUMMARY
    member = (slot // nb) ^ virtual_index(core)
    if group_bits() >= 2:
        member = jnp.where(core == 1, swap_low_bits(member), member)
    key_block = member * nb + slot % nb
    query_block = first_block + jnp.arange(nb, dtype=jnp.int32)
    mask = (key_block[None, :] < query_block[:, None]).astype(jnp.int32)
    mask = jnp.repeat(mask, 8, axis=0)

    attended, dq, dkw, dvw, parts = attention(qb, kb, vb, gb, all_sum, mask)
    att_tok, dq_tok = to_token_layout([attended, dq], core)

    own_grad = reduce_blocks(parts, core).reshape(-1, heads, 2, HEAD_DIM)
    dk = dkw.at[positions].add(own_grad[:, :, 0].reshape(-1, half))
    dv = dvw.at[positions].add(own_grad[:, :, 1].reshape(-1, half))
    dk_tok, dv_tok = to_token_layout([dk.astype(jnp.bfloat16), dv.astype(jnp.bfloat16)], core)
    return att_tok, dq_tok, dk_tok, dv_tok


def solution(mesh):
    seq_size, head_size = mesh.devices.shape
    split = Mesh(mesh.devices.reshape(seq_size, head_size // 2, 2), ("seq", "hx", "hc"))
    tok = P(("seq", "hx", "hc"), None)
    return jax.shard_map(
        body,
        mesh=split,
        in_specs=(tok, tok, tok, tok, P("seq", None)),
        out_specs=(tok, tok, tok, tok),
        check_vma=False,
    )
```

```python
import math

import jax
import jax.numpy as jnp
from jax import lax
from jax.experimental import pallas as pl
from jax.experimental.pallas import tpu as pltpu
from jax.sharding import Mesh
from jax.sharding import PartitionSpec as P

HEAD_DIM = 128
BLOCK = 128
SUMMARY = 8

MASKED_SCORE = -1e30
GROUP = ("seq", "hx")
HEADS_PER_STEP = 4


def group_size():
    return lax.axis_size("seq") * lax.axis_size("hx")


def group_bits():
    size = group_size()
    bits = size.bit_length() - 1
    assert 1 << bits == size
    return bits


def physical_bit(core, bit):
    if core == 1 and group_bits() >= 2 and bit < 2:
        return 1 - bit
    return bit


def exchange(x, mask):
    size = group_size()
    pairs = []
    for g in range(size):
        for c in range(2):
            phys = 0
            for bit in range(group_bits()):
                if (mask >> bit) & 1:
                    phys |= 1 << physical_bit(c, bit)
            pairs.append((g * 2 + c, (g ^ phys) * 2 + c))
    return lax.ppermute(x, ("seq", "hx", "hc"), pairs)


def rounds():
    bits = list(range(group_bits()))
    return [tuple(bits[i:i + 2]) for i in range(0, len(bits), 2)]


def round_index(me, bits):
    return sum(((me >> b) & 1) << i for i, b in enumerate(bits))


def round_mask(m, bits):
    return sum(((m >> i) & 1) << b for i, b in enumerate(bits))


def swap_low_bits(index):
    return (index & ~3) | ((index & 1) << 1) | ((index >> 1) & 1)


def virtual_index(core):
    g = lax.axis_index("seq") * lax.axis_size("hx") + lax.axis_index("hx")
    if group_bits() < 2:
        return g
    return jnp.where(core == 1, swap_low_bits(g), g)


def gather_blocks(x, core):
    held = x[None]
    for bits in reversed(rounds()):
        width = 1 << len(bits)
        got = [held] + [exchange(held, round_mask(m, bits)) for m in range(1, width)]
        held = jnp.stack(got, 1).reshape((-1,) + x.shape)
    return held.reshape((-1,) + x.shape[1:])


def reduce_blocks(x, core):
    size = group_size()
    held = x.reshape((size, -1) + x.shape[1:])
    for bits in rounds():
        width = 1 << len(bits)
        parts = held.reshape((held.shape[0] // width, width) + held.shape[1:])
        total = parts[:, 0]
        for m in range(1, width):
            got = exchange(parts[:, m].astype(jnp.bfloat16), round_mask(m, bits))
            total = total + got.astype(jnp.float32)
        held = total
    return held.reshape(x.shape[0] // size, *x.shape[1:])


def swap_with_partner(x):
    return lax.ppermute(x, "hc", [(0, 1), (1, 0)])


def to_block_layout(arrays, core):
    rows, feats = arrays[0].shape
    half = feats // 2
    mine = [lax.dynamic_slice_in_dim(a, core * half, half, 1) for a in arrays]
    theirs = [lax.dynamic_slice_in_dim(a, (1 - core) * half, half, 1) for a in arrays]
    got = swap_with_partner(jnp.concatenate(theirs, axis=1))
    out = []
    for i, m in enumerate(mine):
        r = got[:, i * half:(i + 1) * half]
        out.append(jnp.where(core == 0, jnp.concatenate([m, r], 0), jnp.concatenate([r, m], 0)))
    return out


def to_token_layout(arrays, core):
    rows2, half = arrays[0].shape
    rows = rows2 // 2
    mine = [lax.dynamic_slice_in_dim(a, core * rows, rows, 0) for a in arrays]
    theirs = [lax.dynamic_slice_in_dim(a, (1 - core) * rows, rows, 0) for a in arrays]
    got = swap_with_partner(jnp.concatenate(theirs, axis=1))
    out = []
    for i, m in enumerate(mine):
        r = got[:, i * half:(i + 1) * half]
        out.append(jnp.where(core == 0, jnp.concatenate([m, r], 1), jnp.concatenate([r, m], 1)))
    return out


def mm(a, b, trans_a=False, trans_b=False):
    dims = (((0 if trans_a else 1,), (1 if trans_b else 0,)), ((), ()))
    return lax.dot_general(a, b, dims, preferred_element_type=jnp.float32)


def attention_kernel(
    q_all, k_all, v_all, g_all, s_all, mask_ref, att_all, dq_all, dkw_all, dvw_all, ds_all
):
    j = pl.program_id(1)
    scale = 1.0 / math.sqrt(HEAD_DIM)
    f32 = jnp.float32
    bf16 = jnp.bfloat16
    allowed = mask_ref[0:1, :] > 0
    row = lax.broadcasted_iota(jnp.int32, (BLOCK, BLOCK), 0)
    col = lax.broadcasted_iota(jnp.int32, (BLOCK, BLOCK), 1)
    causal = row >= col
    for hh in range(q_all.shape[1] // HEAD_DIM):
        cols = pl.ds(hh * HEAD_DIM, HEAD_DIM)
        q = q_all[:, cols]
        k = k_all[:, cols]
        v = v_all[:, cols]
        g = g_all[:, cols]
        sk = s_all[:, pl.ds(2 * hh * HEAD_DIM, HEAD_DIM)]
        sv = s_all[:, pl.ds((2 * hh + 1) * HEAD_DIM, HEAD_DIM)]

        sw = jnp.where(causal, mm(q, k, trans_b=True) * scale, MASKED_SCORE)
        ss = jnp.where(allowed, mm(q, sk, trans_b=True) * scale, MASKED_SCORE)
        fold = sw
        for c in range(ss.shape[1] // BLOCK):
            fold = jnp.maximum(fold, ss[:, c * BLOCK:(c + 1) * BLOCK])
        top = jnp.max(fold, axis=1, keepdims=True)
        ew = jnp.exp(sw - top)
        es = jnp.exp(ss - top)
        fold = ew
        for c in range(es.shape[1] // BLOCK):
            fold = fold + es[:, c * BLOCK:(c + 1) * BLOCK]
        inv = 1.0 / jnp.sum(fold, axis=1, keepdims=True)
        pw = ew * inv
        ps = es * inv
        pw_low = pw.astype(bf16)
        ps_low = ps.astype(bf16)
        att = (mm(pw_low, v) + mm(ps_low, sv)).astype(bf16)
        att_all[:, cols] = att
        delta = jnp.sum(g.astype(f32) * att.astype(f32), axis=1, keepdims=True)
        dsw = (pw * (mm(g, v, trans_b=True) - delta)).astype(bf16)
        dss = (ps * (mm(g, sv, trans_b=True) - delta)).astype(bf16)
        dq_all[:, cols] = ((mm(dsw, k) + mm(dss, sk)) * scale).astype(bf16)
        dkw_all[:, cols] = mm(dsw, q, trans_a=True) * scale
        dvw_all[:, cols] = mm(pw_low, g, trans_a=True)
        dks = mm(dss, q, trans_a=True) * scale
        dvs = mm(ps_low, g, trans_a=True)
        kcols = pl.ds(2 * hh * HEAD_DIM, HEAD_DIM)
        vcols = pl.ds((2 * hh + 1) * HEAD_DIM, HEAD_DIM)

        @pl.when(j == 0)
        def _():
            ds_all[:, kcols] = dks
            ds_all[:, vcols] = dvs

        @pl.when(j > 0)
        def _():
            ds_all[:, kcols] += dks
            ds_all[:, vcols] += dvs


def attention(q, k, v, g, summary, mask):
    rows, half = q.shape
    heads = half // HEAD_DIM
    nb = rows // BLOCK
    count = summary.shape[0]
    per_step = math.gcd(heads, HEADS_PER_STEP)
    tile = pl.BlockSpec((BLOCK, per_step * HEAD_DIM), lambda h, j: (j, h))
    pair = pl.BlockSpec((count, 2 * per_step * HEAD_DIM), lambda h, j: (0, h))
    bf16 = jnp.bfloat16
    f32 = jnp.float32
    flops = 2 * rows * heads * HEAD_DIM * (BLOCK + count) * 6
    return pl.pallas_call(
        attention_kernel,
        grid=(heads // per_step, nb),
        in_specs=[tile, tile, tile, tile, pair, pl.BlockSpec((8, count), lambda h, j: (j, 0))],
        out_specs=[tile, tile, tile, tile, pair],
        out_shape=[
            jax.ShapeDtypeStruct((rows, half), bf16),
            jax.ShapeDtypeStruct((rows, half), bf16),
            jax.ShapeDtypeStruct((rows, half), f32),
            jax.ShapeDtypeStruct((rows, half), f32),
            jax.ShapeDtypeStruct((count, 2 * half), f32),
        ],
        cost_estimate=pl.CostEstimate(
            flops=flops, transcendentals=rows * heads * (BLOCK + count) * 2,
            bytes_accessed=rows * half * 2 * 8 + count * half * 2 * 6,
        ),
    )(q, k, v, g, summary, mask)


def body(queries, key_rows, value_rows, out_grad, summary_columns):
    core = lax.axis_index("hc")
    hx = lax.axis_index("hx")
    shard = lax.axis_index("seq")
    score_scale = 1.0 / math.sqrt(HEAD_DIM)
    f32 = jnp.float32

    qb, kb, vb, gb = to_block_layout([queries, key_rows, value_rows, out_grad], core)
    rows, half = qb.shape
    heads = half // HEAD_DIM
    nb = rows // BLOCK
    pair_count = summary_columns.shape[0] // nb
    first_block = (shard * pair_count + hx) * nb
    cols = lax.dynamic_slice_in_dim(summary_columns, hx * nb, nb, 0)
    positions = (jnp.arange(nb, dtype=jnp.int32)[:, None] * BLOCK + cols).reshape(-1)

    own_sum = jnp.stack(
        [
            jnp.take(kb, positions, axis=0).reshape(-1, heads, HEAD_DIM),
            jnp.take(vb, positions, axis=0).reshape(-1, heads, HEAD_DIM),
        ],
        axis=2,
    ).reshape(-1, 2 * half)
    all_sum = gather_blocks(own_sum, core)
    sum_count = all_sum.shape[0]
    slot = jnp.arange(sum_count, dtype=jnp.int32) // SUMMARY
    member = (slot // nb) ^ virtual_index(core)
    if group_bits() >= 2:
        member = jnp.where(core == 1, swap_low_bits(member), member)
    key_block = member * nb + slot % nb
    query_block = first_block + jnp.arange(nb, dtype=jnp.int32)
    mask = (key_block[None, :] < query_block[:, None]).astype(jnp.int32)
    mask = jnp.repeat(mask, 8, axis=0)

    attended, dq, dkw, dvw, parts = attention(qb, kb, vb, gb, all_sum, mask)
    att_tok, dq_tok = to_token_layout([attended, dq], core)

    own_grad = reduce_blocks(parts, core).reshape(-1, heads, 2, HEAD_DIM)
    place = (jnp.arange(rows, dtype=jnp.int32)[:, None] == positions[None, :]).astype(jnp.float32)
    exact = lax.Precision.HIGHEST
    dk = dkw + jnp.dot(place, own_grad[:, :, 0].reshape(-1, half), precision=exact)
    dv = dvw + jnp.dot(place, own_grad[:, :, 1].reshape(-1, half), precision=exact)
    dk_tok, dv_tok = to_token_layout([dk.astype(jnp.bfloat16), dv.astype(jnp.bfloat16)], core)
    return att_tok, dq_tok, dk_tok, dv_tok


def solution(mesh):
    seq_size, head_size = mesh.devices.shape
    split = Mesh(mesh.devices.reshape(seq_size, head_size // 2, 2), ("seq", "hx", "hc"))
    tok = P(("seq", "hx", "hc"), None)
    return jax.shard_map(
        body,
        mesh=split,
        in_specs=(tok, tok, tok, tok, P("seq", None)),
        out_specs=(tok, tok, tok, tok),
        check_vma=False,
    )
```

```python
import math

import jax
import jax.numpy as jnp
from jax import lax
from jax.experimental import pallas as pl
from jax.experimental.pallas import tpu as pltpu
from jax.sharding import Mesh
from jax.sharding import PartitionSpec as P

HEAD_DIM = 128
BLOCK = 128
SUMMARY = 8

MASKED_SCORE = -1e30
GROUP = ("seq", "hx")
HEADS_PER_STEP = 4


def group_size():
    return lax.axis_size("seq") * lax.axis_size("hx")


def group_bits():
    size = group_size()
    bits = size.bit_length() - 1
    assert 1 << bits == size
    return bits


def physical_bit(core, bit):
    if core == 1 and group_bits() >= 2 and bit < 2:
        return 1 - bit
    return bit


def exchange(x, mask):
    size = group_size()
    pairs = []
    for g in range(size):
        for c in range(2):
            phys = 0
            for bit in range(group_bits()):
                if (mask >> bit) & 1:
                    phys |= 1 << physical_bit(c, bit)
            pairs.append((g * 2 + c, (g ^ phys) * 2 + c))
    return lax.ppermute(x, ("seq", "hx", "hc"), pairs)


def rounds():
    bits = list(range(group_bits()))
    return [tuple(bits[i:i + 2]) for i in range(0, len(bits), 2)]


def round_index(me, bits):
    return sum(((me >> b) & 1) << i for i, b in enumerate(bits))


def round_mask(m, bits):
    return sum(((m >> i) & 1) << b for i, b in enumerate(bits))


def swap_low_bits(index):
    return (index & ~3) | ((index & 1) << 1) | ((index >> 1) & 1)


def virtual_index(core):
    g = lax.axis_index("seq") * lax.axis_size("hx") + lax.axis_index("hx")
    if group_bits() < 2:
        return g
    return jnp.where(core == 1, swap_low_bits(g), g)


def gather_blocks(x, core):
    held = x[None]
    for bits in reversed(rounds()):
        width = 1 << len(bits)
        got = [held] + [exchange(held, round_mask(m, bits)) for m in range(1, width)]
        held = jnp.stack(got, 1).reshape((-1,) + x.shape)
    return held.reshape((-1,) + x.shape[1:])


def reduce_blocks(x, core):
    size = group_size()
    held = x.reshape((size, -1) + x.shape[1:])
    for bits in rounds():
        width = 1 << len(bits)
        parts = held.reshape((held.shape[0] // width, width) + held.shape[1:])
        total = parts[:, 0]
        for m in range(1, width):
            got = exchange(parts[:, m].astype(jnp.bfloat16), round_mask(m, bits))
            total = total + got.astype(jnp.float32)
        held = total
    return held.reshape(x.shape[0] // size, *x.shape[1:])


def swap_with_partner(x):
    return lax.ppermute(x, "hc", [(0, 1), (1, 0)])


def to_block_layout(arrays, core):
    rows, feats = arrays[0].shape
    half = feats // 2
    mine = [lax.dynamic_slice_in_dim(a, core * half, half, 1) for a in arrays]
    theirs = [lax.dynamic_slice_in_dim(a, (1 - core) * half, half, 1) for a in arrays]
    got = swap_with_partner(jnp.concatenate(theirs, axis=1))
    out = []
    for i, m in enumerate(mine):
        r = got[:, i * half:(i + 1) * half]
        out.append(jnp.concatenate([m, r], 0))
    return out


def to_token_layout(arrays, core):
    rows2, half = arrays[0].shape
    rows = rows2 // 2
    mine = [a[:rows] for a in arrays]
    theirs = [a[rows:] for a in arrays]
    got = swap_with_partner(jnp.concatenate(theirs, axis=1))
    out = []
    for i, m in enumerate(mine):
        r = got[:, i * half:(i + 1) * half]
        out.append(jnp.where(core == 0, jnp.concatenate([m, r], 1), jnp.concatenate([r, m], 1)))
    return out


def mm(a, b, trans_a=False, trans_b=False):
    dims = (((0 if trans_a else 1,), (1 if trans_b else 0,)), ((), ()))
    return lax.dot_general(a, b, dims, preferred_element_type=jnp.float32)


def attention_kernel(
    q_all, k_all, v_all, g_all, s_all, mask_ref, row_ref, col_ref, att_all, dq_all, dkw_all, dvw_all, ds_all
):
    j = pl.program_id(1)
    scale = 1.0 / math.sqrt(HEAD_DIM)
    f32 = jnp.float32
    bf16 = jnp.bfloat16
    allowed = mask_ref[0:1, :] > 0
    causal = row_ref[:, 0:1] >= col_ref[0:1, :]
    for hh in range(q_all.shape[1] // HEAD_DIM):
        cols = pl.ds(hh * HEAD_DIM, HEAD_DIM)
        q = q_all[:, cols]
        k = k_all[:, cols]
        v = v_all[:, cols]
        g = g_all[:, cols]
        sk = s_all[:, pl.ds(2 * hh * HEAD_DIM, HEAD_DIM)]
        sv = s_all[:, pl.ds((2 * hh + 1) * HEAD_DIM, HEAD_DIM)]

        sw = jnp.where(causal, mm(q, k, trans_b=True) * scale, MASKED_SCORE)
        ss = jnp.where(allowed, mm(q, sk, trans_b=True) * scale, MASKED_SCORE)
        fold = sw
        for c in range(ss.shape[1] // BLOCK):
            fold = jnp.maximum(fold, ss[:, c * BLOCK:(c + 1) * BLOCK])
        top = jnp.max(fold, axis=1, keepdims=True)
        ew = jnp.exp(sw - top)
        es = jnp.exp(ss - top)
        fold = ew
        for c in range(es.shape[1] // BLOCK):
            fold = fold + es[:, c * BLOCK:(c + 1) * BLOCK]
        inv = 1.0 / jnp.sum(fold, axis=1, keepdims=True)
        pw = ew * inv
        ps = es * inv
        pw_low = pw.astype(bf16)
        ps_low = ps.astype(bf16)
        att = (mm(pw_low, v) + mm(ps_low, sv)).astype(bf16)
        att_all[:, cols] = att
        delta = jnp.sum(g.astype(f32) * att.astype(f32), axis=1, keepdims=True)
        dsw = (pw * (mm(g, v, trans_b=True) - delta)).astype(bf16)
        dss = (ps * (mm(g, sv, trans_b=True) - delta)).astype(bf16)
        dq_all[:, cols] = ((mm(dsw, k) + mm(dss, sk)) * scale).astype(bf16)
        dkw_all[:, cols] = mm(dsw, q, trans_a=True) * scale
        dvw_all[:, cols] = mm(pw_low, g, trans_a=True)
        dks = mm(dss, q, trans_a=True) * scale
        dvs = mm(ps_low, g, trans_a=True)
        kcols = pl.ds(2 * hh * HEAD_DIM, HEAD_DIM)
        vcols = pl.ds((2 * hh + 1) * HEAD_DIM, HEAD_DIM)

        @pl.when(j == 0)
        def _():
            ds_all[:, kcols] = dks
            ds_all[:, vcols] = dvs

        @pl.when(j > 0)
        def _():
            ds_all[:, kcols] += dks
            ds_all[:, vcols] += dvs


def attention(q, k, v, g, summary, mask, row_offset, col_offset):
    rows, half = q.shape
    heads = half // HEAD_DIM
    nb = rows // BLOCK
    count = summary.shape[0]
    per_step = math.gcd(heads, HEADS_PER_STEP)
    tile = pl.BlockSpec((BLOCK, per_step * HEAD_DIM), lambda h, j: (j, h))
    pair = pl.BlockSpec((count, 2 * per_step * HEAD_DIM), lambda h, j: (0, h))
    bf16 = jnp.bfloat16
    f32 = jnp.float32
    flops = 2 * rows * heads * HEAD_DIM * (BLOCK + count) * 6
    return pl.pallas_call(
        attention_kernel,
        grid=(heads // per_step, nb),
        in_specs=[
            tile, tile, tile, tile, pair,
            pl.BlockSpec((8, count), lambda h, j: (j, 0)),
            pl.BlockSpec((BLOCK, BLOCK), lambda h, j: (j, 0)),
            pl.BlockSpec((8, BLOCK), lambda h, j: (j, 0)),
        ],
        out_specs=[tile, tile, tile, tile, pair],
        out_shape=[
            jax.ShapeDtypeStruct((rows, half), bf16),
            jax.ShapeDtypeStruct((rows, half), bf16),
            jax.ShapeDtypeStruct((rows, half), f32),
            jax.ShapeDtypeStruct((rows, half), f32),
            jax.ShapeDtypeStruct((count, 2 * half), f32),
        ],
        cost_estimate=pl.CostEstimate(
            flops=flops, transcendentals=rows * heads * (BLOCK + count) * 2,
            bytes_accessed=rows * half * 2 * 8 + count * half * 2 * 6,
        ),
    )(q, k, v, g, summary, mask, row_offset, col_offset)


def body(queries, key_rows, value_rows, out_grad, summary_columns):
    core = lax.axis_index("hc")
    hx = lax.axis_index("hx")
    shard = lax.axis_index("seq")
    score_scale = 1.0 / math.sqrt(HEAD_DIM)
    f32 = jnp.float32

    qb, kb, vb, gb = to_block_layout([queries, key_rows, value_rows, out_grad], core)
    rows, half = qb.shape
    heads = half // HEAD_DIM
    nb = rows // BLOCK
    pair_count = summary_columns.shape[0] // nb
    first_block = (shard * pair_count + hx) * nb
    cols = lax.dynamic_slice_in_dim(summary_columns, hx * nb, nb, 0)
    true_positions = (jnp.arange(nb, dtype=jnp.int32)[:, None] * BLOCK + cols).reshape(-1)
    own_rows = queries.shape[0]
    positions = (true_positions - core * own_rows) % rows
    true_row = (jnp.arange(rows, dtype=jnp.int32) + core * own_rows) % rows
    in_block = true_row % BLOCK
    row_offset = jnp.broadcast_to(in_block[:, None], (rows, BLOCK))
    col_offset = jnp.repeat(in_block.reshape(nb, BLOCK), 8, axis=0)

    own_sum = jnp.stack(
        [
            jnp.take(kb, positions, axis=0).reshape(-1, heads, HEAD_DIM),
            jnp.take(vb, positions, axis=0).reshape(-1, heads, HEAD_DIM),
        ],
        axis=2,
    ).reshape(-1, 2 * half)
    all_sum = gather_blocks(own_sum, core)
    sum_count = all_sum.shape[0]
    slot = jnp.arange(sum_count, dtype=jnp.int32) // SUMMARY
    member = (slot // nb) ^ virtual_index(core)
    if group_bits() >= 2:
        member = jnp.where(core == 1, swap_low_bits(member), member)
    key_block = member * nb + slot % nb
    query_block = first_block + true_row.reshape(nb, BLOCK)[:, 0] // BLOCK
    mask = (key_block[None, :] < query_block[:, None]).astype(jnp.int32)
    mask = jnp.repeat(mask, 8, axis=0)

    attended, dq, dkw, dvw, parts = attention(qb, kb, vb, gb, all_sum, mask, row_offset, col_offset)
    att_tok, dq_tok = to_token_layout([attended, dq], core)

    own_grad = reduce_blocks(parts, core).reshape(-1, heads, 2, HEAD_DIM)
    place = (jnp.arange(rows, dtype=jnp.int32)[:, None] == positions[None, :]).astype(jnp.float32)
    exact = lax.Precision.HIGHEST
    dk = dkw + jnp.dot(place, own_grad[:, :, 0].reshape(-1, half), precision=exact)
    dv = dvw + jnp.dot(place, own_grad[:, :, 1].reshape(-1, half), precision=exact)
    dk_tok, dv_tok = to_token_layout([dk.astype(jnp.bfloat16), dv.astype(jnp.bfloat16)], core)
    return att_tok, dq_tok, dk_tok, dv_tok


def solution(mesh):
    seq_size, head_size = mesh.devices.shape
    split = Mesh(mesh.devices.reshape(seq_size, head_size // 2, 2), ("seq", "hx", "hc"))
    tok = P(("seq", "hx", "hc"), None)
    return jax.shard_map(
        body,
        mesh=split,
        in_specs=(tok, tok, tok, tok, P("seq", None)),
        out_specs=(tok, tok, tok, tok),
        check_vma=False,
    )
```

```python
import math

import jax
import jax.numpy as jnp
from jax import lax
from jax.experimental import pallas as pl
from jax.experimental.pallas import tpu as pltpu
from jax.sharding import Mesh
from jax.sharding import PartitionSpec as P

HEAD_DIM = 128
BLOCK = 128
SUMMARY = 8

MASKED_SCORE = -1e30
GROUP = ("seq", "hx")
HEADS_PER_STEP = 4


def group_size():
    return lax.axis_size("seq") * lax.axis_size("hx")


def group_bits():
    size = group_size()
    bits = size.bit_length() - 1
    assert 1 << bits == size
    return bits


def physical_bit(core, bit):
    if core == 1 and group_bits() >= 2 and bit < 2:
        return 1 - bit
    return bit


def exchange(x, mask):
    size = group_size()
    pairs = []
    for g in range(size):
        for c in range(2):
            phys = 0
            for bit in range(group_bits()):
                if (mask >> bit) & 1:
                    phys |= 1 << physical_bit(c, bit)
            pairs.append((g * 2 + c, (g ^ phys) * 2 + c))
    return lax.ppermute(x, ("seq", "hx", "hc"), pairs)


def rounds():
    bits = list(range(group_bits()))
    return [tuple(bits[i:i + 2]) for i in range(0, len(bits), 2)]


def round_index(me, bits):
    return sum(((me >> b) & 1) << i for i, b in enumerate(bits))


def round_mask(m, bits):
    return sum(((m >> i) & 1) << b for i, b in enumerate(bits))


def swap_low_bits(index):
    return (index & ~3) | ((index & 1) << 1) | ((index >> 1) & 1)


def virtual_index(core):
    g = lax.axis_index("seq") * lax.axis_size("hx") + lax.axis_index("hx")
    if group_bits() < 2:
        return g
    return jnp.where(core == 1, swap_low_bits(g), g)


def gather_blocks(x, core):
    held = x[None]
    for bits in reversed(rounds()):
        width = 1 << len(bits)
        got = [held] + [exchange(held, round_mask(m, bits)) for m in range(1, width)]
        held = jnp.stack(got, 1).reshape((-1,) + x.shape)
    return held.reshape((-1,) + x.shape[1:])


def reduce_blocks(x, core):
    size = group_size()
    held = x.reshape((size, -1) + x.shape[1:])
    for bits in rounds():
        width = 1 << len(bits)
        parts = held.reshape((held.shape[0] // width, width) + held.shape[1:])
        total = parts[:, 0]
        for m in range(1, width):
            got = exchange(parts[:, m].astype(jnp.bfloat16), round_mask(m, bits))
            total = total + got.astype(jnp.float32)
        held = total
    return held.reshape(x.shape[0] // size, *x.shape[1:])


def swap_with_partner(x):
    return lax.ppermute(x, "hc", [(0, 1), (1, 0)])


def to_block_layout(arrays, core):
    rows, feats = arrays[0].shape
    half = feats // 2
    mine = [lax.dynamic_slice_in_dim(a, core * half, half, 1) for a in arrays]
    theirs = [lax.dynamic_slice_in_dim(a, (1 - core) * half, half, 1) for a in arrays]
    got = swap_with_partner(jnp.concatenate(theirs, axis=1))
    out = []
    for i, m in enumerate(mine):
        r = got[:, i * half:(i + 1) * half]
        out.append(jnp.where(core == 0, jnp.concatenate([m, r], 0), jnp.concatenate([r, m], 0)))
    return out


def to_token_layout(arrays, core):
    rows2, half = arrays[0].shape
    rows = rows2 // 2
    mine = [lax.dynamic_slice_in_dim(a, core * rows, rows, 0) for a in arrays]
    theirs = [lax.dynamic_slice_in_dim(a, (1 - core) * rows, rows, 0) for a in arrays]
    got = swap_with_partner(jnp.concatenate(theirs, axis=1))
    out = []
    for i, m in enumerate(mine):
        r = got[:, i * half:(i + 1) * half]
        out.append(jnp.where(core == 0, jnp.concatenate([m, r], 1), jnp.concatenate([r, m], 1)))
    return out


def mm(a, b, trans_a=False, trans_b=False):
    dims = (((0 if trans_a else 1,), (1 if trans_b else 0,)), ((), ()))
    return lax.dot_general(a, b, dims, preferred_element_type=jnp.float32)


def attention_kernel(
    q_all, k_all, v_all, g_all, s_all, mask_ref, att_all, dq_all, dkw_all, dvw_all, ds_all
):
    j = pl.program_id(1)
    scale = 1.0 / math.sqrt(HEAD_DIM)
    f32 = jnp.float32
    bf16 = jnp.bfloat16
    allowed = mask_ref[0:1, :] > 0
    row = lax.broadcasted_iota(jnp.int32, (BLOCK, BLOCK), 0)
    col = lax.broadcasted_iota(jnp.int32, (BLOCK, BLOCK), 1)
    causal = row >= col
    for hh in range(q_all.shape[1] // HEAD_DIM):
        cols = pl.ds(hh * HEAD_DIM, HEAD_DIM)
        q = q_all[:, cols]
        k = k_all[:, cols]
        v = v_all[:, cols]
        g = g_all[:, cols]
        sk = s_all[:, pl.ds(2 * hh * HEAD_DIM, HEAD_DIM)]
        sv = s_all[:, pl.ds((2 * hh + 1) * HEAD_DIM, HEAD_DIM)]

        sw = jnp.where(causal, mm(q, k, trans_b=True) * scale, MASKED_SCORE)
        ss = jnp.where(allowed, mm(q, sk, trans_b=True) * scale, MASKED_SCORE)
        fold = sw
        for c in range(ss.shape[1] // BLOCK):
            fold = jnp.maximum(fold, ss[:, c * BLOCK:(c + 1) * BLOCK])
        top = jnp.max(fold, axis=1, keepdims=True)
        ew = jnp.exp(sw - top)
        es = jnp.exp(ss - top)
        fold = ew
        for c in range(es.shape[1] // BLOCK):
            fold = fold + es[:, c * BLOCK:(c + 1) * BLOCK]
        inv = 1.0 / jnp.sum(fold, axis=1, keepdims=True)
        pw = ew * inv
        ps = es * inv
        pw_low = pw.astype(bf16)
        ps_low = ps.astype(bf16)
        att = (mm(pw_low, v) + mm(ps_low, sv)).astype(bf16)
        att_all[:, cols] = att
        delta = jnp.sum(g.astype(f32) * att.astype(f32), axis=1, keepdims=True)
        dsw = (pw * (mm(g, v, trans_b=True) - delta)).astype(bf16)
        dss = (ps * (mm(g, sv, trans_b=True) - delta)).astype(bf16)
        dq_all[:, cols] = ((mm(dsw, k) + mm(dss, sk)) * scale).astype(bf16)
        dkw_all[:, cols] = mm(dsw, q, trans_a=True) * scale
        dvw_all[:, cols] = mm(pw_low, g, trans_a=True)
        dks = mm(dss, q, trans_a=True) * scale
        dvs = mm(ps_low, g, trans_a=True)
        kcols = pl.ds(2 * hh * HEAD_DIM, HEAD_DIM)
        vcols = pl.ds((2 * hh + 1) * HEAD_DIM, HEAD_DIM)

        @pl.when(j == 0)
        def _():
            ds_all[:, kcols] = dks
            ds_all[:, vcols] = dvs

        @pl.when(j > 0)
        def _():
            ds_all[:, kcols] += dks
            ds_all[:, vcols] += dvs


def attention(q, k, v, g, summary, mask):
    rows, half = q.shape
    heads = half // HEAD_DIM
    nb = rows // BLOCK
    count = summary.shape[0]
    per_step = math.gcd(heads, HEADS_PER_STEP)
    tile = pl.BlockSpec((BLOCK, per_step * HEAD_DIM), lambda h, j: (j, h))
    pair = pl.BlockSpec((count, 2 * per_step * HEAD_DIM), lambda h, j: (0, h))
    bf16 = jnp.bfloat16
    f32 = jnp.float32
    flops = 2 * rows * heads * HEAD_DIM * (BLOCK + count) * 6
    return pl.pallas_call(
        attention_kernel,
        grid=(heads // per_step, nb),
        in_specs=[tile, tile, tile, tile, pair, pl.BlockSpec((8, count), lambda h, j: (j, 0))],
        out_specs=[tile, tile, tile, tile, pair],
        out_shape=[
            jax.ShapeDtypeStruct((rows, half), bf16),
            jax.ShapeDtypeStruct((rows, half), bf16),
            jax.ShapeDtypeStruct((rows, half), f32),
            jax.ShapeDtypeStruct((rows, half), f32),
            jax.ShapeDtypeStruct((count, 2 * half), f32),
        ],
        cost_estimate=pl.CostEstimate(
            flops=flops, transcendentals=rows * heads * (BLOCK + count) * 2,
            bytes_accessed=rows * half * 2 * 8 + count * half * 2 * 6,
        ),
    )(q, k, v, g, summary, mask)


def body(queries, key_rows, value_rows, out_grad, summary_columns):
    core = lax.axis_index("hc")
    hx = lax.axis_index("hx")
    shard = lax.axis_index("seq")
    score_scale = 1.0 / math.sqrt(HEAD_DIM)
    f32 = jnp.float32

    qb, kb, vb, gb = to_block_layout([queries, key_rows, value_rows, out_grad], core)
    rows, half = qb.shape
    heads = half // HEAD_DIM
    nb = rows // BLOCK
    pair_count = summary_columns.shape[0] // nb
    first_block = (shard * pair_count + hx) * nb
    cols = lax.dynamic_slice_in_dim(summary_columns, hx * nb, nb, 0)
    positions = (jnp.arange(nb, dtype=jnp.int32)[:, None] * BLOCK + cols).reshape(-1)

    chosen = (positions[:, None] == jnp.arange(rows, dtype=jnp.int32)[None, :]).astype(jnp.bfloat16)

    def pick(x):
        return jnp.dot(chosen, x, preferred_element_type=jnp.float32).astype(jnp.bfloat16)

    own_sum = jnp.stack(
        [
            pick(kb).reshape(-1, heads, HEAD_DIM),
            pick(vb).reshape(-1, heads, HEAD_DIM),
        ],
        axis=2,
    ).reshape(-1, 2 * half)
    all_sum = gather_blocks(own_sum, core)
    sum_count = all_sum.shape[0]
    slot = jnp.arange(sum_count, dtype=jnp.int32) // SUMMARY
    member = (slot // nb) ^ virtual_index(core)
    if group_bits() >= 2:
        member = jnp.where(core == 1, swap_low_bits(member), member)
    key_block = member * nb + slot % nb
    query_block = first_block + jnp.arange(nb, dtype=jnp.int32)
    mask = (key_block[None, :] < query_block[:, None]).astype(jnp.int32)
    mask = jnp.repeat(mask, 8, axis=0)

    attended, dq, dkw, dvw, parts = attention(qb, kb, vb, gb, all_sum, mask)
    att_tok, dq_tok = to_token_layout([attended, dq], core)

    own_grad = reduce_blocks(parts, core).reshape(-1, heads, 2, HEAD_DIM)
    place = (jnp.arange(rows, dtype=jnp.int32)[:, None] == positions[None, :]).astype(jnp.float32)
    exact = lax.Precision.HIGHEST
    dk = dkw + jnp.dot(place, own_grad[:, :, 0].reshape(-1, half), precision=exact)
    dv = dvw + jnp.dot(place, own_grad[:, :, 1].reshape(-1, half), precision=exact)
    dk_tok, dv_tok = to_token_layout([dk.astype(jnp.bfloat16), dv.astype(jnp.bfloat16)], core)
    return att_tok, dq_tok, dk_tok, dv_tok


def solution(mesh):
    seq_size, head_size = mesh.devices.shape
    split = Mesh(mesh.devices.reshape(seq_size, head_size // 2, 2), ("seq", "hx", "hc"))
    tok = P(("seq", "hx", "hc"), None)
    return jax.shard_map(
        body,
        mesh=split,
        in_specs=(tok, tok, tok, tok, P("seq", None)),
        out_specs=(tok, tok, tok, tok),
        check_vma=False,
    )
```
